128 devices in a mesh: gx: 8 (over y, core), gy: 16 (over z, x).
Axes of the slice: x: 4, y: 4, z: 4, core: 2. Of those that a mesh axis runs over, the one named last changes fastest.
Arguments:
- later_adjoint: bfloat16 [16, 64, 2, 192, 512], P('gx', 'gy'), may hold values from -6 to 6
- coupling: bfloat16 [16, 64, 2, 6, 192, 48], P('gx', 'gy'), may hold values from -0.375 to 0.375
- inverse_diag: bfloat16 [16, 64, 2, 192, 192], P('gx', 'gy'), may hold values from -0.2 to 1.2
- tile_mask: int32 [16, 64, 2, 6], P('gx', 'gy'), may hold values 0 or 1
- perf_cell: int32 [128, 256], P(('gx', 'gy')), may hold values from 0 to 1023
- perf_slot: int32 [128, 256], P(('gx', 'gy')), may hold values from 0 to 23
- perf_live: int32 [128, 256], P(('gx', 'gy')), may hold values from 0 to 1, as said below
- perf_coef: float32 [3, 128, 256], P(None, ('gx', 'gy')), may hold values from -1.2 to 1.2
- well_gain: float32 [3072], P(('gx', 'gy')), may hold values from 0.3 to 1.5
- misfit: float32 [2, 3072, 512], P(None, ('gx', 'gy')), may hold values from -6 to 6
Outputs:
- earlier_adjoint: bfloat16 [16, 64, 2, 192, 512], P('gx', 'gy')
- well_adjoint: bfloat16 [2, 3072, 512], P(None, ('gx', 'gy'))
The draws below stay inside these ranges and needn't reach their ends.
Inputs may be any that keep to these rules, and one draw needn't show every extreme that they name: `perf_live`: some owner receives only used slots from every device.
All inputs are finite; a program needn't handle non-finite values. No bound on the sum of `tile_mask` on one device may be relied on, other than what follows from the above.
Results may differ from the reference program's by a relative error of at most 0.0015.
The reference program's roundings to bfloat16 on the way (of `adjoint`, `faces`, `message` and `source`) count: a program that leaves them out, or rounds other values in their place, can miss the bound.
Values may be sent and summed in bfloat16 or wider, within the bound.
No kernel may reach another device: no remote copies, remote signals or barrier semaphores. Data moves between devices by JAX's collectives and lax.ppermute only.
A program may use at most 128 MiB of HBM per device.

```python
import math
import jax
import jax.numpy as jnp
from jax import lax

TILES_X = 2
TILES_Y = 4
TILES_Z = 2
ADJOINTS = 512
WELLS_DEV = 24
CAPACITY = 2
STEPS = 2
UNKNOWNS = 192
FACE_ROWS = 48
GRID_X = 16
GRID_Y = 64
CELLS_DEV = 1024
SLOTS = 256
WELLS = 3072
N_GX = 8
N_GY = 16


def draw_inverse_diag(key, part):
    shape = (GRID_X, GRID_Y, TILES_Z, UNKNOWNS, UNKNOWNS)
    spread = 0.6 / UNKNOWNS ** 0.5
    noise = jax.random.truncated_normal(key, -4.0, 4.0, shape, jnp.float32) * spread
    row_ids = jnp.arange(UNKNOWNS, dtype=jnp.int32)[:, None]
    col_ids = jnp.arange(UNKNOWNS, dtype=jnp.int32)[None, :]
    identity = jnp.where(row_ids == col_ids, 1.0, 0.0).astype(jnp.float32)
    return (identity + noise).astype(jnp.bfloat16)


def draw_perf_live(key, part):
    owners = SLOTS // CAPACITY
    level_key = jax.random.fold_in(key, 11)
    hot_key = jax.random.fold_in(key, 12)
    slot_key = jax.random.fold_in(key, 13)
    levels = jax.random.randint(level_key, (owners,), 1, 5)
    hottest = jax.random.randint(hot_key, (), 0, owners)
    levels = jnp.where(jnp.arange(owners, dtype=jnp.int32) == hottest, 4, levels)
    owner_of_slot = jnp.arange(SLOTS, dtype=jnp.int32) // CAPACITY
    rolls = jax.random.randint(slot_key, (owners, SLOTS), 0, 4)
    return jnp.where(rolls < levels[owner_of_slot][None, :], 1, 0).astype(jnp.int32)


def place_ends(result, stream_key, low, high):
    longest = result.shape.index(max(result.shape))
    spots = []
    for shift in (0, 1):
        where = [jax.random.randint(jax.random.fold_in(stream_key, axis), (), 0, length) for axis, length in enumerate(result.shape)]
        where[longest] = (where[longest] + shift) % result.shape[longest]
        spots.append(tuple(where))
    return result.at[spots[0]].set(low).at[spots[1]].set(high)


def level_of(own_key, shape, cuts, smallest, largest):
    def one(axis_at, shards_of):
        heights = jax.random.uniform(jax.random.fold_in(jax.random.fold_in(own_key, 6), axis_at), (shards_of,), jnp.float32, smallest / len(cuts), largest / len(cuts))
        return jnp.repeat(jnp.exp(heights), shape[axis_at] // shards_of).reshape((-1,) + (1,) * (len(shape) - axis_at - 1))

    gain = one(*cuts[0])
    for cut in cuts[1:]:
        gain = gain * one(*cut)
    return gain


def normal_values(own_key, shape, scale, reach, cuts=(), kind=jnp.bfloat16):
    result = scale * jax.random.normal(own_key, shape, jnp.float32)
    if cuts:
        result = result * level_of(own_key, shape, cuts, -0.22, 0.18)
    return jnp.clip(result, -reach, reach).astype(kind)


def setup_inputs(seed: int = 0) -> dict:
    arg_keys = jax.random.split(jax.random.key(seed), 11)
    later_adjoint = normal_values(arg_keys[0], (GRID_X, GRID_Y, TILES_Z, UNKNOWNS, ADJOINTS), 1.0, 6.0, ((0, 8), (1, 16)))
    coupling = normal_values(arg_keys[1], (GRID_X, GRID_Y, TILES_Z, 6, UNKNOWNS, FACE_ROWS), (6 * FACE_ROWS) ** -0.5, 0.375, ((0, 8), (1, 16)))
    inverse_diag = draw_inverse_diag(jax.random.fold_in(arg_keys[10], 71), 0)
    tile_mask = place_ends((jax.random.randint(arg_keys[3], (GRID_X, GRID_Y, TILES_Z, 6), 0, 8) < 7).astype(jnp.int32), jax.random.fold_in(arg_keys[3], 1), 0, 1)
    perf_cell = place_ends(jax.random.randint(arg_keys[4], (N_GX * N_GY, SLOTS), 0, CELLS_DEV), jax.random.fold_in(arg_keys[4], 1), 0, CELLS_DEV - 1).astype(jnp.int32)
    perf_slot = place_ends(jax.random.randint(arg_keys[5], (N_GX * N_GY, SLOTS), 0, WELLS_DEV), jax.random.fold_in(arg_keys[5], 1), 0, WELLS_DEV - 1).astype(jnp.int32)
    perf_live = draw_perf_live(jax.random.fold_in(arg_keys[10], 71), 0)
    perf_coef = jnp.clip(jax.random.uniform(arg_keys[7], (3, N_GX * N_GY, SLOTS), jnp.float32, -1.2, 1.2) * level_of(arg_keys[7], (3, N_GX * N_GY, SLOTS), ((1, 128),), -0.4, 0.0), -1.2, 1.2)
    well_gain = jnp.clip(jnp.exp(math.log(1.5) - 1.60943787 * jax.random.uniform(arg_keys[8], (WELLS,), jnp.float32) ** level_of(arg_keys[8], (WELLS,), ((0, 128),), -0.2, 0.2)), 0.3, 1.5)
    misfit = normal_values(arg_keys[9], (STEPS, WELLS, ADJOINTS), 1.0, 6.0, ((1, 128),), jnp.float32)
    return {"later_adjoint": later_adjoint, "coupling": coupling, "inverse_diag": inverse_diag, "tile_mask": tile_mask, "perf_cell": perf_cell, "perf_slot": perf_slot, "perf_live": perf_live, "perf_coef": perf_coef, "well_gain": well_gain, "misfit": misfit}


def neighbour(values, axis, offset):
    extent = values.shape[axis]
    widths = [(0, 0)] * values.ndim
    widths[axis] = (1, 1)
    padded = jnp.pad(values, widths)
    return lax.slice_in_dim(padded, 1 + offset, 1 + offset + extent, axis=axis)


def face_stack(adjoint):
    columns = adjoint.shape[-1]
    cells = adjoint.reshape(GRID_X, GRID_Y, TILES_Z, 3, 4, 4, 4, columns)
    lower_x = neighbour(cells, 0, -1)[:, :, :, :, 3]
    upper_x = neighbour(cells, 0, 1)[:, :, :, :, 0]
    lower_y = neighbour(cells, 1, -1)[:, :, :, :, :, 3]
    upper_y = neighbour(cells, 1, 1)[:, :, :, :, :, 0]
    lower_z = neighbour(cells, 2, -1)[:, :, :, :, :, :, 3]
    upper_z = neighbour(cells, 2, 1)[:, :, :, :, :, :, 0]
    listed = [lower_x, upper_x, lower_y, upper_y, lower_z, upper_z]
    listed = [face.reshape(GRID_X, GRID_Y, TILES_Z, 48, columns) for face in listed]
    return jnp.stack(listed, axis=3)


def to_devices(values):
    columns = values.shape[-1]
    shaped = values.reshape(N_GX, TILES_X, N_GY, TILES_Y, TILES_Z, 192, columns)
    return shaped.transpose(0, 2, 1, 3, 4, 5, 6).reshape(N_GX * N_GY, TILES_X * TILES_Y * TILES_Z * 192, columns)


def from_devices(values):
    columns = values.shape[-1]
    shaped = values.reshape(N_GX, N_GY, TILES_X, TILES_Y, TILES_Z, 192, columns)
    return shaped.transpose(0, 2, 1, 3, 4, 5, 6).reshape(GRID_X, GRID_Y, TILES_Z, 192, columns)


def sweep(adjoint, misfit_step, coupling, inverse_diag, tile_mask, perf_cell, perf_slot, perf_live, perf_coef, well_gain):
    columns = adjoint.shape[-1]
    device_count = N_GX * N_GY
    faces = face_stack(adjoint) * tile_mask[..., None, None].astype(jnp.bfloat16)
    flux = jnp.einsum('abcdij,abcdjr->abcir', coupling.astype(jnp.float32), faces.astype(jnp.float32))
    adjoint_dev = to_devices(adjoint)
    flux_dev = to_devices(flux)
    tile_of = perf_cell // 64
    cell_of = perf_cell % 64
    in_use = perf_live.astype(jnp.float32)[:, :, None]
    message = jnp.zeros((device_count, SLOTS, columns), jnp.float32)
    row_list = []
    for component in range(3):
        row_index = (tile_of * 192 + component * 64 + cell_of).astype(jnp.int32)
        picked = jnp.take_along_axis(adjoint_dev, row_index[:, :, None], axis=1).astype(jnp.float32)
        message = message + perf_coef[component][:, :, None] * picked
        row_list.append(row_index)
    message = (in_use * message).astype(jnp.bfloat16)
    owner = (jnp.arange(SLOTS, dtype=jnp.int32) // CAPACITY)[None, :]
    well_id = (owner * WELLS_DEV + perf_slot).astype(jnp.int32).reshape(-1)
    summed = jax.ops.segment_sum(message.reshape(-1, columns).astype(jnp.float32), well_id, num_segments=WELLS)
    well_adj = (well_gain[:, None] * (summed + misfit_step)).astype(jnp.bfloat16)
    returned = well_adj[well_id].reshape(device_count, SLOTS, columns).astype(jnp.float32) * in_use
    device_ids = jnp.arange(device_count, dtype=jnp.int32)[:, None]
    for component in range(3):
        flux_dev = flux_dev.at[device_ids, row_list[component]].add(perf_coef[component][:, :, None] * returned)
    source = from_devices(flux_dev).astype(jnp.bfloat16)
    updated = -jnp.einsum('abcij,abcjr->abcir', inverse_diag.astype(jnp.float32), source.astype(jnp.float32))
    return updated.astype(jnp.bfloat16), well_adj


def reference(later_adjoint, coupling, inverse_diag, tile_mask, perf_cell, perf_slot, perf_live, perf_coef, well_gain, misfit):
    block_cols = min(ADJOINTS, 128)
    blocks = ADJOINTS // block_cols
    adjoint_blocks = later_adjoint.reshape(GRID_X, GRID_Y, TILES_Z, 192, blocks, block_cols).transpose(4, 0, 1, 2, 3, 5)
    misfit_blocks = misfit.reshape(STEPS, WELLS, blocks, block_cols).transpose(2, 0, 1, 3)

    def solve_block(block_pair):
        adjoint, misfit_block = block_pair
        collected = []
        for sweep_index in range(STEPS):
            adjoint, well_adj = sweep(adjoint, misfit_block[sweep_index], coupling, inverse_diag, tile_mask,
                                      perf_cell, perf_slot, perf_live, perf_coef, well_gain)
            collected.append(well_adj)
        return adjoint, jnp.stack(collected)

    adjoint_out, wells_out = lax.map(solve_block, (adjoint_blocks, misfit_blocks))
    earlier = adjoint_out.transpose(1, 2, 3, 4, 0, 5).reshape(GRID_X, GRID_Y, TILES_Z, 192, ADJOINTS)
    well_adjoint = wells_out.transpose(1, 2, 0, 3).reshape(STEPS, WELLS, ADJOINTS)
    return earlier, well_adjoint
```

```python
import numpy as np
import jax
import jax.numpy as jnp
from jax import lax
from jax.experimental import pallas as pl
from jax.experimental.pallas import tpu as pltpu
from jax.sharding import PartitionSpec as P


CAPACITY = 2
STEPS = 2
F32 = jnp.float32
BF16 = jnp.bfloat16


def face_rows():
    rows = np.zeros((6, 48), np.int32)
    for k in range(3):
        for p in range(4):
            for q in range(4):
                f = 16 * k + 4 * p + q
                rows[0, f] = 64 * k + 16 * 3 + 4 * p + q
                rows[1, f] = 64 * k + 4 * p + q
                rows[2, f] = 64 * k + 16 * p + 4 * 3 + q
                rows[3, f] = 64 * k + 16 * p + q
                rows[4, f] = 64 * k + 16 * p + 4 * q + 3
                rows[5, f] = 64 * k + 16 * p + 4 * q
    return rows


FACE_ROWS = face_rows()


def selection():
    sel = np.zeros((6, 48, 192), np.float32)
    for d in range(6):
        sel[d, np.arange(48), FACE_ROWS[d]] = 1.0
    return sel


def halo_faces(adjoint):
    sx, sy, sz, _, cols = adjoint.shape
    cells = adjoint.reshape(sx, sy, sz, 3, 4, 4, 4, cols)
    to_up_x = cells[sx - 1, :, :, :, 3].reshape(sy * sz, 48, cols)
    to_down_x = cells[0, :, :, :, 0].reshape(sy * sz, 48, cols)
    to_up_y = cells[:, sy - 1, :, :, :, 3].reshape(sx * sz, 48, cols)
    to_down_y = cells[:, 0, :, :, :, 0].reshape(sx * sz, 48, cols)
    out = []
    for axis, up_part, down_part in (("gx", to_up_x, to_down_x), ("gy", to_up_y, to_down_y)):
        count = lax.axis_size(axis)
        up = [(i, i + 1) for i in range(count - 1)]
        down = [(j, i) for i, j in up]
        out.append(lax.ppermute(up_part, axis, up))
        out.append(lax.ppermute(down_part, axis, down))
    return out


def make_step_kernel(sx, sy, sz, with_message):
    per_x = sy * sz

    def kernel(a_ref, hxm_ref, hxp_ref, hym_ref, hyp_ref, coup_ref, sel_ref,
               phi_ref, plo_ref, landed_ref, inv_ref, pthi_ref, ptlo_ref,
               out_ref, *rest):
        if with_message:
            msg_ref, faces_ref, acc_ref = rest
        else:
            (faces_ref,) = rest
        t = pl.program_id(0)
        a = t // per_x
        b = (t // sz) % sy
        c = t % sz

        def put(d, value):
            faces_ref[pl.ds(48 * d, 48), :] = value

        def inner(d, nb):
            put(d, jnp.dot(sel_ref[d], a_ref[nb], preferred_element_type=F32).astype(BF16))

        zero = jnp.zeros((48, a_ref.shape[-1]), BF16)
        neighbours = (
            (a > 0, t - per_x, hxm_ref, b * sz + c),
            (a < sx - 1, t + per_x, hxp_ref, b * sz + c),
            (b > 0, t - sz, hym_ref, a * sz + c),
            (b < sy - 1, t + sz, hyp_ref, a * sz + c),
            (c > 0, t - 1, None, None),
            (c < sz - 1, t + 1, None, None),
        )
        for d, (inside, nb, halo, slot) in enumerate(neighbours):
            nb = jnp.clip(nb, 0, sx * sy * sz - 1)

            @pl.when(inside)
            def _():
                inner(d, nb)

            @pl.when(jnp.logical_not(inside))
            def _():
                if halo is None:
                    put(d, zero)
                else:
                    put(d, halo[slot])

        flux = jnp.dot(coup_ref[0], faces_ref[...], preferred_element_type=F32)
        landed = landed_ref[...]
        added = jnp.dot(phi_ref[0], landed, preferred_element_type=F32)
        added = added + jnp.dot(plo_ref[0], landed, preferred_element_type=F32)
        source = (flux + added).astype(BF16)
        new = (-jnp.dot(inv_ref[0], source, preferred_element_type=F32)).astype(BF16)
        out_ref[0] = new
        if with_message:
            part = jnp.dot(pthi_ref[0], new, preferred_element_type=F32)
            part = part + jnp.dot(ptlo_ref[0], new, preferred_element_type=F32)

            @pl.when(t == 0)
            def _():
                acc_ref[...] = part

            @pl.when(t > 0)
            def _():
                acc_ref[...] += part

            @pl.when(t == pl.num_programs(0) - 1)
            def _():
                msg_ref[...] = acc_ref[...].astype(BF16)

    return kernel


def step_call(adjoint, halos, coup, sel, p_hi, p_lo, landed, inv, pt_hi, pt_lo, with_message):
    sx, sy, sz, rows, cols = adjoint.shape
    tiles = sx * sy * sz
    slots = landed.shape[0]
    flat = adjoint.reshape(tiles, rows, cols)
    full3 = lambda shape: pl.BlockSpec(shape, lambda t: (0, 0, 0))
    full2 = lambda shape: pl.BlockSpec(shape, lambda t: (0, 0))
    tile3 = lambda shape: pl.BlockSpec((1,) + shape, lambda t: (t, 0, 0))
    in_specs = [
        full3((tiles, rows, cols)),
        full3(halos[0].shape),
        full3(halos[1].shape),
        full3(halos[2].shape),
        full3(halos[3].shape),
        tile3(coup.shape[1:]),
        full3(sel.shape),
        tile3(p_hi.shape[1:]),
        tile3(p_lo.shape[1:]),
        full2(landed.shape),
        tile3(inv.shape[1:]),
        tile3(pt_hi.shape[1:]),
        tile3(pt_lo.shape[1:]),
    ]
    out_shape = [jax.ShapeDtypeStruct((tiles, rows, cols), BF16)]
    out_specs = [tile3((rows, cols))]
    scratch = [pltpu.VMEM((6 * 48, cols), BF16)]
    if with_message:
        out_shape.append(jax.ShapeDtypeStruct((slots, cols), BF16))
        out_specs.append(full2((slots, cols)))
        scratch.append(pltpu.VMEM((slots, cols), F32))
    result = pl.pallas_call(
        make_step_kernel(sx, sy, sz, with_message),
        grid=(tiles,),
        in_specs=in_specs,
        out_specs=out_specs,
        out_shape=out_shape,
        scratch_shapes=scratch,
        compiler_params=pltpu.CompilerParams(
            dimension_semantics=("arbitrary",), vmem_limit_bytes=48 * 1024 * 1024
        ),
    )(flat, *halos, coup, sel, p_hi, p_lo, landed, inv, pt_hi, pt_lo)
    new = result[0].reshape(adjoint.shape)
    message = result[1] if with_message else None
    return new, message


def split(values):
    hi = values.astype(BF16)
    lo = (values - hi.astype(F32)).astype(BF16)
    return hi, lo


def local(
    later_adjoint,
    coupling,
    inverse_diag,
    tile_mask,
    perf_cell,
    perf_slot,
    perf_live,
    perf_coef,
    well_gain,
    misfit,
):
    sx, sy, sz, rows, cols = later_adjoint.shape
    tiles = sx * sy * sz
    slot_count = perf_cell.shape[1]
    peers = slot_count // CAPACITY
    wells_here = well_gain.shape[0]
    axes = ("gx", "gy")

    mask = tile_mask.astype(BF16).reshape(tiles, 6)
    coup = coupling.reshape(tiles, 6, rows, 48) * mask[:, :, None, None]
    coup = coup.transpose(0, 2, 1, 3).reshape(tiles, rows, 6 * 48)
    inv = inverse_diag.reshape(tiles, rows, rows)
    sel = jnp.asarray(selection(), BF16)

    in_use = perf_live[0].astype(F32)
    cell_ids = perf_cell[0]
    tile_of = cell_ids // 64
    cell_of = cell_ids % 64
    tile_ids = jnp.arange(tiles, dtype=jnp.int32)[:, None, None]
    unk_ids = jnp.arange(rows, dtype=jnp.int32)[None, :, None]
    place = jnp.zeros((tiles, rows, slot_count), F32)
    for component in range(3):
        hit = (tile_ids == tile_of[None, None, :]) & (unk_ids == (component * 64 + cell_of)[None, None, :])
        place = place + jnp.where(hit, (perf_coef[component, 0] * in_use)[None, None, :], 0.0)
    p_hi, p_lo = split(place)
    pt_hi = p_hi.transpose(0, 2, 1)
    pt_lo = p_lo.transpose(0, 2, 1)

    slot_tag = perf_slot[0].astype(BF16).reshape(peers, CAPACITY)
    arrived_tags = lax.all_to_all(slot_tag, axes, split_axis=0, concat_axis=0, tiled=True)
    well_index = jnp.arange(wells_here, dtype=jnp.int32).astype(BF16)
    selector = (arrived_tags.reshape(1, slot_count) == well_index[:, None]).astype(BF16)

    adjoint = later_adjoint
    flat0 = later_adjoint.reshape(tiles, rows, cols)
    message = (
        jnp.einsum("tup,tuc->pc", p_hi, flat0, preferred_element_type=F32)
        + jnp.einsum("tup,tuc->pc", p_lo, flat0, preferred_element_type=F32)
    ).astype(BF16)
    collected = []
    for sweep_index in range(STEPS):
        halos = halo_faces(adjoint)
        arrived = lax.all_to_all(
            message.reshape(peers, CAPACITY, cols), axes, split_axis=0, concat_axis=0, tiled=True
        )
        summed = jnp.dot(selector, arrived.reshape(slot_count, cols), preferred_element_type=F32)
        well_adj = (well_gain[:, None] * (summed + misfit[sweep_index])).astype(BF16)
        returned = jnp.einsum("ws,wr->sr", selector, well_adj, preferred_element_type=F32).astype(BF16)
        landed = lax.all_to_all(
            returned.reshape(peers, CAPACITY, cols), axes, split_axis=0, concat_axis=0, tiled=True
        ).reshape(slot_count, cols)
        last = sweep_index == STEPS - 1
        adjoint, message = step_call(
            adjoint, halos, coup, sel, p_hi, p_lo, landed, inv, pt_hi, pt_lo, not last
        )
        collected.append(well_adj)
    return (adjoint, jnp.stack(collected))


def solution(mesh):
    return jax.shard_map(
        local,
        mesh=mesh,
        in_specs=(
            P("gx", "gy", None, None, None),
            P("gx", "gy", None, None, None, None),
            P("gx", "gy", None, None, None),
            P("gx", "gy", None, None),
            P(("gx", "gy"), None),
            P(("gx", "gy"), None),
            P(("gx", "gy"), None),
            P(None, ("gx", "gy"), None),
            P(("gx", "gy")),
            P(None, ("gx", "gy"), None),
        ),
        out_specs=(P("gx", "gy", None, None, None), P(None, ("gx", "gy"), None)),
        check_vma=False,
    )
```

```python
import numpy as np
import jax
import jax.numpy as jnp
from jax import lax
from jax.experimental import pallas as pl
from jax.experimental.pallas import tpu as pltpu
from jax.sharding import PartitionSpec as P


CAPACITY = 2
STEPS = 2
F32 = jnp.float32
BF16 = jnp.bfloat16


def face_rows():
    rows = np.zeros((6, 48), np.int32)
    for k in range(3):
        for p in range(4):
            for q in range(4):
                f = 16 * k + 4 * p + q
                rows[0, f] = 64 * k + 16 * 3 + 4 * p + q
                rows[1, f] = 64 * k + 4 * p + q
                rows[2, f] = 64 * k + 16 * p + 4 * 3 + q
                rows[3, f] = 64 * k + 16 * p + q
                rows[4, f] = 64 * k + 16 * p + 4 * q + 3
                rows[5, f] = 64 * k + 16 * p + 4 * q
    return rows


FACE_ROWS = face_rows()


def selection():
    sel = np.zeros((6, 48, 192), np.float32)
    for d in range(6):
        sel[d, np.arange(48), FACE_ROWS[d]] = 1.0
    return sel


def halo_faces(adjoint):
    sx, sy, sz, _, cols = adjoint.shape
    cells = adjoint.reshape(sx, sy, sz, 3, 4, 4, 4, cols)
    to_up_x = cells[sx - 1, :, :, :, 3].reshape(sy * sz, 48, cols)
    to_down_x = cells[0, :, :, :, 0].reshape(sy * sz, 48, cols)
    to_up_y = cells[:, sy - 1, :, :, :, 3].reshape(sx * sz, 48, cols)
    to_down_y = cells[:, 0, :, :, :, 0].reshape(sx * sz, 48, cols)
    out = []
    for axis, up_part, down_part in (("gx", to_up_x, to_down_x), ("gy", to_up_y, to_down_y)):
        count = lax.axis_size(axis)
        up = [(i, i + 1) for i in range(count - 1)]
        down = [(j, i) for i, j in up]
        out.append(lax.ppermute(up_part, axis, up))
        out.append(lax.ppermute(down_part, axis, down))
    return out


def make_step_kernel(sx, sy, sz, with_message):
    per_x = sy * sz

    def kernel(a_ref, hxm_ref, hxp_ref, hym_ref, hyp_ref, coup_ref, sel_ref,
               phi_ref, plo_ref, landed_ref, inv_ref, pthi_ref, ptlo_ref,
               out_ref, *rest):
        if with_message:
            msg_ref, faces_ref, acc_ref = rest
        else:
            (faces_ref,) = rest
        t = pl.program_id(0)
        a = t // per_x
        b = (t // sz) % sy
        c = t % sz

        def put(d, value):
            faces_ref[pl.ds(48 * d, 48), :] = value

        def inner(d, nb):
            put(d, jnp.dot(sel_ref[d], a_ref[nb], preferred_element_type=F32).astype(BF16))

        zero = jnp.zeros((48, a_ref.shape[-1]), BF16)
        neighbours = (
            (a > 0, t - per_x, hxm_ref, b * sz + c),
            (a < sx - 1, t + per_x, hxp_ref, b * sz + c),
            (b > 0, t - sz, hym_ref, a * sz + c),
            (b < sy - 1, t + sz, hyp_ref, a * sz + c),
            (c > 0, t - 1, None, None),
            (c < sz - 1, t + 1, None, None),
        )
        for d, (inside, nb, halo, slot) in enumerate(neighbours):
            nb = jnp.clip(nb, 0, sx * sy * sz - 1)

            @pl.when(inside)
            def _():
                inner(d, nb)

            @pl.when(jnp.logical_not(inside))
            def _():
                if halo is None:
                    put(d, zero)
                else:
                    put(d, halo[slot])

        flux = jnp.dot(coup_ref[0], faces_ref[...], preferred_element_type=F32)
        landed = landed_ref[...]
        added = jnp.dot(phi_ref[0], landed, preferred_element_type=F32)
        added = added + jnp.dot(plo_ref[0], landed, preferred_element_type=F32)
        source = (flux + added).astype(BF16)
        new = (-jnp.dot(inv_ref[0], source, preferred_element_type=F32)).astype(BF16)
        out_ref[0] = new
        if with_message:
            part = jnp.dot(pthi_ref[0], new, preferred_element_type=F32)
            part = part + jnp.dot(ptlo_ref[0], new, preferred_element_type=F32)

            @pl.when(t == 0)
            def _():
                acc_ref[...] = part

            @pl.when(t > 0)
            def _():
                acc_ref[...] += part

            @pl.when(t == pl.num_programs(0) - 1)
            def _():
                msg_ref[...] = acc_ref[...].astype(BF16)

    return kernel


def step_call(adjoint, halos, coup, sel, p_hi, p_lo, landed, inv, pt_hi, pt_lo, with_message):
    sx, sy, sz, rows, cols = adjoint.shape
    tiles = sx * sy * sz
    slots = landed.shape[0]
    flat = adjoint.reshape(tiles, rows, cols)
    full3 = lambda shape: pl.BlockSpec(shape, lambda t: (0, 0, 0))
    full2 = lambda shape: pl.BlockSpec(shape, lambda t: (0, 0))
    tile3 = lambda shape: pl.BlockSpec((1,) + shape, lambda t: (t, 0, 0))
    in_specs = [
        full3((tiles, rows, cols)),
        full3(halos[0].shape),
        full3(halos[1].shape),
        full3(halos[2].shape),
        full3(halos[3].shape),
        tile3(coup.shape[1:]),
        full3(sel.shape),
        tile3(p_hi.shape[1:]),
        tile3(p_lo.shape[1:]),
        full2(landed.shape),
        tile3(inv.shape[1:]),
        tile3(pt_hi.shape[1:]),
        tile3(pt_lo.shape[1:]),
    ]
    out_shape = [jax.ShapeDtypeStruct((tiles, rows, cols), BF16)]
    out_specs = [tile3((rows, cols))]
    scratch = [pltpu.VMEM((6 * 48, cols), BF16)]
    if with_message:
        out_shape.append(jax.ShapeDtypeStruct((slots, cols), BF16))
        out_specs.append(full2((slots, cols)))
        scratch.append(pltpu.VMEM((slots, cols), F32))
    result = pl.pallas_call(
        make_step_kernel(sx, sy, sz, with_message),
        grid=(tiles,),
        in_specs=in_specs,
        out_specs=out_specs,
        out_shape=out_shape,
        scratch_shapes=scratch,
        compiler_params=pltpu.CompilerParams(
            dimension_semantics=("arbitrary",), vmem_limit_bytes=48 * 1024 * 1024
        ),
    )(flat, *halos, coup, sel, p_hi, p_lo, landed, inv, pt_hi, pt_lo)
    new = result[0].reshape(adjoint.shape)
    message = result[1] if with_message else None
    return new, message


def exchange(values):
    count_x, count_y = lax.axis_size("gx"), lax.axis_size("gy")
    shaped = values.reshape((count_x, count_y) + values.shape[1:])
    shaped = lax.all_to_all(shaped, "gx", 0, 0, tiled=True)
    shaped = lax.all_to_all(shaped, "gy", 1, 1, tiled=True)
    return shaped.reshape(values.shape)


def split(values):
    hi = values.astype(BF16)
    lo = (values - hi.astype(F32)).astype(BF16)
    return hi, lo


def local(
    later_adjoint,
    coupling,
    inverse_diag,
    tile_mask,
    perf_cell,
    perf_slot,
    perf_live,
    perf_coef,
    well_gain,
    misfit,
):
    sx, sy, sz, rows, cols = later_adjoint.shape
    tiles = sx * sy * sz
    slot_count = perf_cell.shape[1]
    peers = slot_count // CAPACITY
    wells_here = well_gain.shape[0]
    axes = ("gx", "gy")

    mask = tile_mask.astype(BF16).reshape(tiles, 6)
    coup = coupling.reshape(tiles, 6, rows, 48) * mask[:, :, None, None]
    coup = coup.transpose(0, 2, 1, 3).reshape(tiles, rows, 6 * 48)
    inv = inverse_diag.reshape(tiles, rows, rows)
    sel = jnp.asarray(selection(), BF16)

    in_use = perf_live[0].astype(F32)
    cell_ids = perf_cell[0]
    tile_of = cell_ids // 64
    cell_of = cell_ids % 64
    tile_ids = jnp.arange(tiles, dtype=jnp.int32)[:, None, None]
    unk_ids = jnp.arange(rows, dtype=jnp.int32)[None, :, None]
    place = jnp.zeros((tiles, rows, slot_count), F32)
    for component in range(3):
        hit = (tile_ids == tile_of[None, None, :]) & (unk_ids == (component * 64 + cell_of)[None, None, :])
        place = place + jnp.where(hit, (perf_coef[component, 0] * in_use)[None, None, :], 0.0)
    p_hi, p_lo = split(place)
    pt_hi = p_hi.transpose(0, 2, 1)
    pt_lo = p_lo.transpose(0, 2, 1)

    slot_tag = perf_slot[0].astype(BF16).reshape(peers, CAPACITY, 1)
    well_index = jnp.arange(wells_here, dtype=jnp.int32).astype(BF16)

    adjoint = later_adjoint
    flat0 = later_adjoint.reshape(tiles, rows, cols)
    message = (
        jnp.einsum("tup,tuc->pc", p_hi, flat0, preferred_element_type=F32)
        + jnp.einsum("tup,tuc->pc", p_lo, flat0, preferred_element_type=F32)
    ).astype(BF16)
    collected = []
    for sweep_index in range(STEPS):
        halos = halo_faces(adjoint)
        payload = message.reshape(peers, CAPACITY, cols)
        if sweep_index == 0:
            tags = jnp.broadcast_to(slot_tag, (peers, CAPACITY, 128))
            payload = jnp.concatenate([payload, tags], axis=2)
        arrived = exchange(payload)
        if sweep_index == 0:
            arrived_tags = arrived[:, :, cols]
            selector = (arrived_tags.reshape(1, slot_count) == well_index[:, None]).astype(BF16)
        arrived = arrived[:, :, :cols]
        summed = jnp.dot(selector, arrived.reshape(slot_count, cols), preferred_element_type=F32)
        well_adj = (well_gain[:, None] * (summed + misfit[sweep_index])).astype(BF16)
        returned = jnp.einsum("ws,wr->sr", selector, well_adj, preferred_element_type=F32).astype(BF16)
        landed = exchange(returned.reshape(peers, CAPACITY, cols)).reshape(slot_count, cols)
        last = sweep_index == STEPS - 1
        adjoint, message = step_call(
            adjoint, halos, coup, sel, p_hi, p_lo, landed, inv, pt_hi, pt_lo, not last
        )
        collected.append(well_adj)
    return (adjoint, jnp.stack(collected))


def solution(mesh):
    return jax.shard_map(
        local,
        mesh=mesh,
        in_specs=(
            P("gx", "gy", None, None, None),
            P("gx", "gy", None, None, None, None),
            P("gx", "gy", None, None, None),
            P("gx", "gy", None, None),
            P(("gx", "gy"), None),
            P(("gx", "gy"), None),
            P(("gx", "gy"), None),
            P(None, ("gx", "gy"), None),
            P(("gx", "gy")),
            P(None, ("gx", "gy"), None),
        ),
        out_specs=(P("gx", "gy", None, None, None), P(None, ("gx", "gy"), None)),
        check_vma=False,
    )
```

```python
import numpy as np
import jax
import jax.numpy as jnp
from jax import lax
from jax.experimental import pallas as pl
from jax.experimental.pallas import tpu as pltpu
from jax.sharding import PartitionSpec as P


CAPACITY = 2
STEPS = 2
F32 = jnp.float32
BF16 = jnp.bfloat16


def face_rows():
    rows = np.zeros((6, 48), np.int32)
    for k in range(3):
        for p in range(4):
            for q in range(4):
                f = 16 * k + 4 * p + q
                rows[0, f] = 64 * k + 16 * 3 + 4 * p + q
                rows[1, f] = 64 * k + 4 * p + q
                rows[2, f] = 64 * k + 16 * p + 4 * 3 + q
                rows[3, f] = 64 * k + 16 * p + q
                rows[4, f] = 64 * k + 16 * p + 4 * q + 3
                rows[5, f] = 64 * k + 16 * p + 4 * q
    return rows


FACE_ROWS = face_rows()


def selection():
    sel = np.zeros((6, 48, 192), np.float32)
    for d in range(6):
        sel[d, np.arange(48), FACE_ROWS[d]] = 1.0
    return sel


def halo_faces(adjoint):
    sx, sy, sz, _, cols = adjoint.shape
    cells = adjoint.reshape(sx, sy, sz, 3, 4, 4, 4, cols)
    to_up_x = cells[sx - 1, :, :, :, 3].reshape(sy * sz, 48, cols)
    to_down_x = cells[0, :, :, :, 0].reshape(sy * sz, 48, cols)
    to_up_y = cells[:, sy - 1, :, :, :, 3].reshape(sx * sz, 48, cols)
    to_down_y = cells[:, 0, :, :, :, 0].reshape(sx * sz, 48, cols)
    out = []
    for axis, up_part, down_part in (("gx", to_up_x, to_down_x), ("gy", to_up_y, to_down_y)):
        count = lax.axis_size(axis)
        up = [(i, i + 1) for i in range(count - 1)]
        down = [(j, i) for i, j in up]
        out.append(lax.ppermute(up_part, axis, up))
        out.append(lax.ppermute(down_part, axis, down))
    return out


def make_step_kernel(sx, sy, sz, with_message):
    per_x = sy * sz

    def kernel(a_ref, hxm_ref, hxp_ref, hym_ref, hyp_ref, coup_ref, sel_ref,
               phi_ref, plo_ref, landed_ref, inv_ref, *rest):
        if with_message:
            pthi_ref, ptlo_ref, out_ref, msg_ref, faces_ref, acc_ref = rest
        else:
            out_ref, faces_ref = rest
        t = pl.program_id(0)
        a = t // per_x
        b = (t // sz) % sy
        c = t % sz

        def put(d, value):
            faces_ref[pl.ds(48 * d, 48), :] = value

        def inner(d, nb):
            put(d, jnp.dot(sel_ref[d], a_ref[nb], preferred_element_type=F32).astype(BF16))

        zero = jnp.zeros((48, a_ref.shape[-1]), BF16)
        neighbours = (
            (a > 0, t - per_x, hxm_ref, b * sz + c),
            (a < sx - 1, t + per_x, hxp_ref, b * sz + c),
            (b > 0, t - sz, hym_ref, a * sz + c),
            (b < sy - 1, t + sz, hyp_ref, a * sz + c),
            (c > 0, t - 1, None, None),
            (c < sz - 1, t + 1, None, None),
        )
        for d, (inside, nb, halo, slot) in enumerate(neighbours):
            nb = jnp.clip(nb, 0, sx * sy * sz - 1)

            @pl.when(inside)
            def _():
                inner(d, nb)

            @pl.when(jnp.logical_not(inside))
            def _():
                if halo is None:
                    put(d, zero)
                else:
                    put(d, halo[slot])

        flux = jnp.dot(coup_ref[0], faces_ref[...], preferred_element_type=F32)
        landed = landed_ref[...]
        added = jnp.dot(phi_ref[0], landed, preferred_element_type=F32)
        added = added + jnp.dot(plo_ref[0], landed, preferred_element_type=F32)
        source = (flux + added).astype(BF16)
        new = (-jnp.dot(inv_ref[0], source, preferred_element_type=F32)).astype(BF16)
        out_ref[0] = new
        if with_message:
            part = jnp.dot(pthi_ref[0], new, preferred_element_type=F32)
            part = part + jnp.dot(ptlo_ref[0], new, preferred_element_type=F32)

            @pl.when(t == 0)
            def _():
                acc_ref[...] = part

            @pl.when(t > 0)
            def _():
                acc_ref[...] += part

            @pl.when(t == pl.num_programs(0) - 1)
            def _():
                msg_ref[...] = acc_ref[...].astype(BF16)

    return kernel


def step_call(adjoint, halos, coup, sel, p_hi, p_lo, landed, inv, pt_hi, pt_lo, with_message):
    sx, sy, sz, rows, cols = adjoint.shape
    tiles = sx * sy * sz
    slots = landed.shape[0]
    flat = adjoint.reshape(tiles, rows, cols)
    full3 = lambda shape: pl.BlockSpec(shape, lambda t: (0, 0, 0))
    full2 = lambda shape: pl.BlockSpec(shape, lambda t: (0, 0))
    tile3 = lambda shape: pl.BlockSpec((1,) + shape, lambda t: (t, 0, 0))
    in_specs = [
        full3((tiles, rows, cols)),
        full3(halos[0].shape),
        full3(halos[1].shape),
        full3(halos[2].shape),
        full3(halos[3].shape),
        tile3(coup.shape[1:]),
        full3(sel.shape),
        tile3(p_hi.shape[1:]),
        tile3(p_lo.shape[1:]),
        full2(landed.shape),
        tile3(inv.shape[1:]),
    ]
    operands = [flat, *halos, coup, sel, p_hi, p_lo, landed, inv]
    if with_message:
        in_specs += [tile3(pt_hi.shape[1:]), tile3(pt_lo.shape[1:])]
        operands += [pt_hi, pt_lo]
    out_shape = [jax.ShapeDtypeStruct((tiles, rows, cols), BF16)]
    out_specs = [tile3((rows, cols))]
    scratch = [pltpu.VMEM((6 * 48, cols), BF16)]
    if with_message:
        out_shape.append(jax.ShapeDtypeStruct((slots, cols), BF16))
        out_specs.append(full2((slots, cols)))
        scratch.append(pltpu.VMEM((slots, cols), F32))
    result = pl.pallas_call(
        make_step_kernel(sx, sy, sz, with_message),
        grid=(tiles,),
        in_specs=in_specs,
        out_specs=out_specs,
        out_shape=out_shape,
        scratch_shapes=scratch,
        compiler_params=pltpu.CompilerParams(
            dimension_semantics=("arbitrary",), vmem_limit_bytes=48 * 1024 * 1024
        ),
    )(*operands)
    new = result[0].reshape(adjoint.shape)
    message = result[1] if with_message else None
    return new, message


def exchange(values):
    return lax.all_to_all(values, ("gx", "gy"), split_axis=0, concat_axis=0, tiled=True)


def split(values):
    hi = values.astype(BF16)
    lo = (values - hi.astype(F32)).astype(BF16)
    return hi, lo


def local(
    later_adjoint,
    coupling,
    inverse_diag,
    tile_mask,
    perf_cell,
    perf_slot,
    perf_live,
    perf_coef,
    well_gain,
    misfit,
):
    sx, sy, sz, rows, cols = later_adjoint.shape
    tiles = sx * sy * sz
    slot_count = perf_cell.shape[1]
    peers = slot_count // CAPACITY
    wells_here = well_gain.shape[0]
    axes = ("gx", "gy")

    mask = tile_mask.astype(BF16).reshape(tiles, 6)
    coup = coupling.reshape(tiles, 6, rows, 48) * mask[:, :, None, None]
    coup = coup.transpose(0, 2, 1, 3).reshape(tiles, rows, 6 * 48)
    inv = inverse_diag.reshape(tiles, rows, rows)
    sel = jnp.asarray(selection(), BF16)

    in_use = perf_live[0].astype(F32)
    cell_ids = perf_cell[0]
    tile_of = cell_ids // 64
    cell_of = cell_ids % 64
    weights = [perf_coef[component, 0] * in_use for component in range(3)]

    def placement(slot_last):
        tile_ids = jnp.arange(tiles, dtype=jnp.int32)[:, None, None]
        if slot_last:
            unk_ids = jnp.arange(rows, dtype=jnp.int32)[None, :, None]
            pick = lambda v: v[None, None, :]
        else:
            unk_ids = jnp.arange(rows, dtype=jnp.int32)[None, None, :]
            pick = lambda v: v[None, :, None]
        place = 0.0
        for component in range(3):
            hit = (tile_ids == pick(tile_of)) & (unk_ids == pick(component * 64 + cell_of))
            place = place + jnp.where(hit, pick(weights[component]), 0.0)
        return split(place)

    p_hi, p_lo = placement(True)
    pt_hi, pt_lo = placement(False)

    slot_tag = perf_slot[0].astype(BF16).reshape(peers, CAPACITY, 1)
    well_index = jnp.arange(wells_here, dtype=jnp.int32).astype(BF16)

    adjoint = later_adjoint
    flat0 = later_adjoint.reshape(tiles, rows, cols)
    message = (
        jnp.einsum("tup,tuc->pc", p_hi, flat0, preferred_element_type=F32)
        + jnp.einsum("tup,tuc->pc", p_lo, flat0, preferred_element_type=F32)
    ).astype(BF16)
    collected = []
    for sweep_index in range(STEPS):
        halos = halo_faces(adjoint)
        payload = message.reshape(peers, CAPACITY, cols)
        if sweep_index == 0:
            tags = jnp.broadcast_to(slot_tag, (peers, CAPACITY, 128))
            payload = jnp.concatenate([payload, tags], axis=2)
        arrived = exchange(payload)
        if sweep_index == 0:
            arrived_tags = arrived[:, :, cols]
            selector = (arrived_tags.reshape(1, slot_count) == well_index[:, None]).astype(BF16)
        arrived = arrived[:, :, :cols]
        summed = jnp.dot(selector, arrived.reshape(slot_count, cols), preferred_element_type=F32)
        well_adj = (well_gain[:, None] * (summed + misfit[sweep_index])).astype(BF16)
        returned = jnp.einsum("ws,wr->sr", selector, well_adj, preferred_element_type=F32).astype(BF16)
        landed = exchange(returned.reshape(peers, CAPACITY, cols)).reshape(slot_count, cols)
        last = sweep_index == STEPS - 1
        adjoint, message = step_call(
            adjoint, halos, coup, sel, p_hi, p_lo, landed, inv, pt_hi, pt_lo, not last
        )
        collected.append(well_adj)
    return (adjoint, jnp.stack(collected))


def solution(mesh):
    return jax.shard_map(
        local,
        mesh=mesh,
        in_specs=(
            P("gx", "gy", None, None, None),
            P("gx", "gy", None, None, None, None),
            P("gx", "gy", None, None, None),
            P("gx", "gy", None, None),
            P(("gx", "gy"), None),
            P(("gx", "gy"), None),
            P(("gx", "gy"), None),
            P(None, ("gx", "gy"), None),
            P(("gx", "gy")),
            P(None, ("gx", "gy"), None),
        ),
        out_specs=(P("gx", "gy", None, None, None), P(None, ("gx", "gy"), None)),
        check_vma=False,
    )
```

```python
import numpy as np
import jax
import jax.numpy as jnp
from jax import lax
from jax.experimental import pallas as pl
from jax.experimental.pallas import tpu as pltpu
from jax.sharding import PartitionSpec as P


CAPACITY = 2
STEPS = 2
F32 = jnp.float32
BF16 = jnp.bfloat16


def face_rows():
    rows = np.zeros((6, 48), np.int32)
    for k in range(3):
        for p in range(4):
            for q in range(4):
                f = 16 * k + 4 * p + q
                rows[0, f] = 64 * k + 16 * 3 + 4 * p + q
                rows[1, f] = 64 * k + 4 * p + q
                rows[2, f] = 64 * k + 16 * p + 4 * 3 + q
                rows[3, f] = 64 * k + 16 * p + q
                rows[4, f] = 64 * k + 16 * p + 4 * q + 3
                rows[5, f] = 64 * k + 16 * p + 4 * q
    return rows


FACE_ROWS = face_rows()


def selection():
    sel = np.zeros((6, 48, 192), np.float32)
    for d in range(6):
        sel[d, np.arange(48), FACE_ROWS[d]] = 1.0
    return sel


def halo_faces(adjoint):
    sx, sy, sz, _, cols = adjoint.shape
    cells = adjoint.reshape(sx, sy, sz, 3, 4, 4, 4, cols)
    to_up_x = cells[sx - 1, :, :, :, 3].reshape(sy * sz, 48, cols)
    to_down_x = cells[0, :, :, :, 0].reshape(sy * sz, 48, cols)
    to_up_y = cells[:, sy - 1, :, :, :, 3].reshape(sx * sz, 48, cols)
    to_down_y = cells[:, 0, :, :, :, 0].reshape(sx * sz, 48, cols)
    out = []
    for axis, up_part, down_part in (("gx", to_up_x, to_down_x), ("gy", to_up_y, to_down_y)):
        count = lax.axis_size(axis)
        up = [(i, i + 1) for i in range(count - 1)]
        down = [(j, i) for i, j in up]
        out.append(lax.ppermute(up_part, axis, up))
        out.append(lax.ppermute(down_part, axis, down))
    return out


def emit_faces(sel_ref, value, a, b, c, sx, sy, sz, refs):
    ux_ref, dx_ref, uy_ref, dy_ref = refs
    cases = (
        (a == sx - 1, ux_ref, b * sz + c, 0),
        (a == 0, dx_ref, b * sz + c, 1),
        (b == sy - 1, uy_ref, a * sz + c, 2),
        (b == 0, dy_ref, a * sz + c, 3),
    )
    for on_side, ref, slot, d in cases:

        @pl.when(on_side)
        def _():
            ref[slot] = jnp.dot(sel_ref[d], value, preferred_element_type=F32).astype(BF16)


def face_specs(sx, sy, sz, cols):
    shapes = [(sy * sz, 48, cols), (sy * sz, 48, cols), (sx * sz, 48, cols), (sx * sz, 48, cols)]
    specs = [pl.BlockSpec(shape, lambda t: (0, 0, 0)) for shape in shapes]
    return [jax.ShapeDtypeStruct(shape, BF16) for shape in shapes], specs


def faces_kernel(sx, sy, sz):
    def kernel(a_ref, sel_ref, *refs):
        t = pl.program_id(0)
        emit_faces(sel_ref, a_ref[0], t // (sy * sz), (t // sz) % sy, t % sz, sx, sy, sz, refs)

    return kernel


def boundary_faces(adjoint, sel):
    sx, sy, sz, rows, cols = adjoint.shape
    tiles = sx * sy * sz
    shapes, specs = face_specs(sx, sy, sz, cols)
    return pl.pallas_call(
        faces_kernel(sx, sy, sz),
        grid=(tiles,),
        in_specs=[pl.BlockSpec((1, rows, cols), lambda t: (t, 0, 0)), pl.BlockSpec(sel.shape, lambda t: (0, 0, 0))],
        out_specs=specs,
        out_shape=shapes,
        compiler_params=pltpu.CompilerParams(dimension_semantics=("arbitrary",)),
    )(adjoint.reshape(tiles, rows, cols), sel)


def send_faces(faces):
    out = []
    for axis, up_part, down_part in (("gx", faces[0], faces[1]), ("gy", faces[2], faces[3])):
        count = lax.axis_size(axis)
        up = [(i, i + 1) for i in range(count - 1)]
        down = [(j, i) for i, j in up]
        out.append(lax.ppermute(up_part, axis, up))
        out.append(lax.ppermute(down_part, axis, down))
    return out


def make_step_kernel(sx, sy, sz, with_message):
    per_x = sy * sz

    def kernel(a_ref, hxm_ref, hxp_ref, hym_ref, hyp_ref, coup_ref, sel_ref,
               phi_ref, plo_ref, landed_ref, inv_ref, *rest):
        if with_message:
            pthi_ref, ptlo_ref, out_ref, msg_ref, ux_ref, dx_ref, uy_ref, dy_ref, faces_ref, acc_ref = rest
        else:
            out_ref, faces_ref = rest
        t = pl.program_id(0)
        a = t // per_x
        b = (t // sz) % sy
        c = t % sz

        def put(d, value):
            faces_ref[pl.ds(48 * d, 48), :] = value

        def inner(d, nb):
            put(d, jnp.dot(sel_ref[d], a_ref[nb], preferred_element_type=F32).astype(BF16))

        zero = jnp.zeros((48, a_ref.shape[-1]), BF16)
        neighbours = (
            (a > 0, t - per_x, hxm_ref, b * sz + c),
            (a < sx - 1, t + per_x, hxp_ref, b * sz + c),
            (b > 0, t - sz, hym_ref, a * sz + c),
            (b < sy - 1, t + sz, hyp_ref, a * sz + c),
            (c > 0, t - 1, None, None),
            (c < sz - 1, t + 1, None, None),
        )
        for d, (inside, nb, halo, slot) in enumerate(neighbours):
            nb = jnp.clip(nb, 0, sx * sy * sz - 1)

            @pl.when(inside)
            def _():
                inner(d, nb)

            @pl.when(jnp.logical_not(inside))
            def _():
                if halo is None:
                    put(d, zero)
                else:
                    put(d, halo[slot])

        flux = jnp.dot(coup_ref[0], faces_ref[...], preferred_element_type=F32)
        landed = landed_ref[...]
        added = jnp.dot(phi_ref[0], landed, preferred_element_type=F32)
        added = added + jnp.dot(plo_ref[0], landed, preferred_element_type=F32)
        source = (flux + added).astype(BF16)
        new = (-jnp.dot(inv_ref[0], source, preferred_element_type=F32)).astype(BF16)
        out_ref[0] = new
        if with_message:
            part = jnp.dot(pthi_ref[0], new, preferred_element_type=F32)
            part = part + jnp.dot(ptlo_ref[0], new, preferred_element_type=F32)

            emit_faces(sel_ref, new, a, b, c, sx, sy, sz, (ux_ref, dx_ref, uy_ref, dy_ref))

            @pl.when(t == 0)
            def _():
                acc_ref[...] = part

            @pl.when(t > 0)
            def _():
                acc_ref[...] += part

            @pl.when(t == pl.num_programs(0) - 1)
            def _():
                msg_ref[...] = acc_ref[...].astype(BF16)

    return kernel


def step_call(adjoint, halos, coup, sel, p_hi, p_lo, landed, inv, pt_hi, pt_lo, with_message):
    sx, sy, sz, rows, cols = adjoint.shape
    tiles = sx * sy * sz
    slots = landed.shape[0]
    flat = adjoint.reshape(tiles, rows, cols)
    full3 = lambda shape: pl.BlockSpec(shape, lambda t: (0, 0, 0))
    full2 = lambda shape: pl.BlockSpec(shape, lambda t: (0, 0))
    tile3 = lambda shape: pl.BlockSpec((1,) + shape, lambda t: (t, 0, 0))
    in_specs = [
        full3((tiles, rows, cols)),
        full3(halos[0].shape),
        full3(halos[1].shape),
        full3(halos[2].shape),
        full3(halos[3].shape),
        tile3(coup.shape[1:]),
        full3(sel.shape),
        tile3(p_hi.shape[1:]),
        tile3(p_lo.shape[1:]),
        full2(landed.shape),
        tile3(inv.shape[1:]),
    ]
    operands = [flat, *halos, coup, sel, p_hi, p_lo, landed, inv]
    if with_message:
        in_specs += [tile3(pt_hi.shape[1:]), tile3(pt_lo.shape[1:])]
        operands += [pt_hi, pt_lo]
    out_shape = [jax.ShapeDtypeStruct((tiles, rows, cols), BF16)]
    out_specs = [tile3((rows, cols))]
    scratch = [pltpu.VMEM((6 * 48, cols), BF16)]
    if with_message:
        out_shape.append(jax.ShapeDtypeStruct((slots, cols), BF16))
        out_specs.append(full2((slots, cols)))
        shapes, specs = face_specs(sx, sy, sz, cols)
        out_shape += shapes
        out_specs += specs
        scratch.append(pltpu.VMEM((slots, cols), F32))
    result = pl.pallas_call(
        make_step_kernel(sx, sy, sz, with_message),
        grid=(tiles,),
        in_specs=in_specs,
        out_specs=out_specs,
        out_shape=out_shape,
        scratch_shapes=scratch,
        compiler_params=pltpu.CompilerParams(
            dimension_semantics=("arbitrary",), vmem_limit_bytes=48 * 1024 * 1024
        ),
    )(*operands)
    new = result[0].reshape(adjoint.shape)
    if not with_message:
        return new, None, None
    return new, result[1], list(result[2:6])


def exchange(values):
    return lax.all_to_all(values, ("gx", "gy"), split_axis=0, concat_axis=0, tiled=True)


def split(values):
    hi = values.astype(BF16)
    lo = (values - hi.astype(F32)).astype(BF16)
    return hi, lo


def local(
    later_adjoint,
    coupling,
    inverse_diag,
    tile_mask,
    perf_cell,
    perf_slot,
    perf_live,
    perf_coef,
    well_gain,
    misfit,
):
    sx, sy, sz, rows, cols = later_adjoint.shape
    tiles = sx * sy * sz
    slot_count = perf_cell.shape[1]
    peers = slot_count // CAPACITY
    wells_here = well_gain.shape[0]
    axes = ("gx", "gy")

    mask = tile_mask.astype(BF16).reshape(tiles, 6)
    coup = coupling.reshape(tiles, 6, rows, 48) * mask[:, :, None, None]
    coup = coup.transpose(0, 2, 1, 3).reshape(tiles, rows, 6 * 48)
    inv = inverse_diag.reshape(tiles, rows, rows)
    sel = jnp.asarray(selection(), BF16)

    in_use = perf_live[0].astype(F32)
    cell_ids = perf_cell[0]
    tile_of = cell_ids // 64
    cell_of = cell_ids % 64
    weights = [perf_coef[component, 0] * in_use for component in range(3)]

    def placement(slot_last):
        tile_ids = jnp.arange(tiles, dtype=jnp.int32)[:, None, None]
        if slot_last:
            unk_ids = jnp.arange(rows, dtype=jnp.int32)[None, :, None]
            pick = lambda v: v[None, None, :]
        else:
            unk_ids = jnp.arange(rows, dtype=jnp.int32)[None, None, :]
            pick = lambda v: v[None, :, None]
        place = 0.0
        for component in range(3):
            hit = (tile_ids == pick(tile_of)) & (unk_ids == pick(component * 64 + cell_of))
            place = place + jnp.where(hit, pick(weights[component]), 0.0)
        return split(place)

    p_hi, p_lo = placement(True)
    pt_hi, pt_lo = placement(False)

    slot_tag = perf_slot[0].astype(BF16).reshape(peers, CAPACITY, 1)
    well_index = jnp.arange(wells_here, dtype=jnp.int32).astype(BF16)

    adjoint = later_adjoint
    faces = boundary_faces(later_adjoint, sel)
    flat0 = later_adjoint.reshape(tiles, rows, cols)
    message = (
        jnp.einsum("tup,tuc->pc", p_hi, flat0, preferred_element_type=F32)
        + jnp.einsum("tup,tuc->pc", p_lo, flat0, preferred_element_type=F32)
    ).astype(BF16)
    collected = []
    for sweep_index in range(STEPS):
        halos = send_faces(faces)
        payload = message.reshape(peers, CAPACITY, cols)
        if sweep_index == 0:
            tags = jnp.broadcast_to(slot_tag, (peers, CAPACITY, 128))
            payload = jnp.concatenate([payload, tags], axis=2)
        arrived = exchange(payload)
        if sweep_index == 0:
            arrived_tags = arrived[:, :, cols]
            selector = (arrived_tags.reshape(1, slot_count) == well_index[:, None]).astype(BF16)
        arrived = arrived[:, :, :cols]
        summed = jnp.dot(selector, arrived.reshape(slot_count, cols), preferred_element_type=F32)
        well_adj = (well_gain[:, None] * (summed + misfit[sweep_index])).astype(BF16)
        returned = jnp.einsum("ws,wr->sr", selector, well_adj, preferred_element_type=F32).astype(BF16)
        landed = exchange(returned.reshape(peers, CAPACITY, cols)).reshape(slot_count, cols)
        last = sweep_index == STEPS - 1
        adjoint, message, faces = step_call(
            adjoint, halos, coup, sel, p_hi, p_lo, landed, inv, pt_hi, pt_lo, not last
        )
        collected.append(well_adj)
    return (adjoint, jnp.stack(collected))


def solution(mesh):
    return jax.shard_map(
        local,
        mesh=mesh,
        in_specs=(
            P("gx", "gy", None, None, None),
            P("gx", "gy", None, None, None, None),
            P("gx", "gy", None, None, None),
            P("gx", "gy", None, None),
            P(("gx", "gy"), None),
            P(("gx", "gy"), None),
            P(("gx", "gy"), None),
            P(None, ("gx", "gy"), None),
            P(("gx", "gy")),
            P(None, ("gx", "gy"), None),
        ),
        out_specs=(P("gx", "gy", None, None, None), P(None, ("gx", "gy"), None)),
        check_vma=False,
    )
```

```python
import numpy as np
import jax
import jax.numpy as jnp
from jax import lax
from jax.experimental import pallas as pl
from jax.experimental.pallas import tpu as pltpu
from jax.sharding import PartitionSpec as P


CAPACITY = 2
STEPS = 2
F32 = jnp.float32
BF16 = jnp.bfloat16


def face_rows():
    rows = np.zeros((6, 48), np.int32)
    for k in range(3):
        for p in range(4):
            for q in range(4):
                f = 16 * k + 4 * p + q
                rows[0, f] = 64 * k + 16 * 3 + 4 * p + q
                rows[1, f] = 64 * k + 4 * p + q
                rows[2, f] = 64 * k + 16 * p + 4 * 3 + q
                rows[3, f] = 64 * k + 16 * p + q
                rows[4, f] = 64 * k + 16 * p + 4 * q + 3
                rows[5, f] = 64 * k + 16 * p + 4 * q
    return rows


FACE_ROWS = face_rows()


def selection():
    sel = np.zeros((6, 48, 192), np.float32)
    for d in range(6):
        sel[d, np.arange(48), FACE_ROWS[d]] = 1.0
    return sel


def tile_coords(t, sy, sz):
    return t // (sy * sz), (t // sz) % sy, t % sz


def emit_halos(faces, a, b, c, sx, sy, sz, refs):
    ux_ref, dx_ref, uy_ref, dy_ref = refs
    cases = (
        (a == sx - 1, ux_ref, b * sz + c, 0),
        (a == 0, dx_ref, b * sz + c, 1),
        (b == sy - 1, uy_ref, a * sz + c, 2),
        (b == 0, dy_ref, a * sz + c, 3),
    )
    for on_side, ref, slot, d in cases:

        @pl.when(on_side)
        def _():
            ref[slot] = faces[48 * d : 48 * d + 48]


def face_outputs(sx, sy, sz, cols):
    tiles = sx * sy * sz
    shapes = [(sy * sz, 48, cols), (sy * sz, 48, cols), (sx * sz, 48, cols), (sx * sz, 48, cols)]
    specs = [pl.BlockSpec(shape, lambda t: (0, 0, 0)) for shape in shapes]
    out_shape = [jax.ShapeDtypeStruct((tiles, 288, cols), BF16)]
    out_specs = [pl.BlockSpec((1, 288, cols), lambda t: (t, 0, 0))]
    out_shape += [jax.ShapeDtypeStruct(shape, BF16) for shape in shapes]
    return out_shape, out_specs + specs


def faces_kernel(sx, sy, sz):
    def kernel(a_ref, sel_ref, of_ref, *refs):
        t = pl.program_id(0)
        a, b, c = tile_coords(t, sy, sz)
        faces = jnp.dot(sel_ref[...], a_ref[0], preferred_element_type=F32).astype(BF16)
        of_ref[0] = faces
        emit_halos(faces, a, b, c, sx, sy, sz, refs)

    return kernel


def all_faces(adjoint, sel):
    sx, sy, sz, rows, cols = adjoint.shape
    tiles = sx * sy * sz
    out_shape, out_specs = face_outputs(sx, sy, sz, cols)
    result = pl.pallas_call(
        faces_kernel(sx, sy, sz),
        grid=(tiles,),
        in_specs=[pl.BlockSpec((1, rows, cols), lambda t: (t, 0, 0)), pl.BlockSpec(sel.shape, lambda t: (0, 0))],
        out_specs=out_specs,
        out_shape=out_shape,
        compiler_params=pltpu.CompilerParams(dimension_semantics=("arbitrary",)),
    )(adjoint.reshape(tiles, rows, cols), sel)
    return result[0], list(result[1:])


def send_faces(sides):
    out = []
    for axis, up_part, down_part in (("gx", sides[0], sides[1]), ("gy", sides[2], sides[3])):
        count = lax.axis_size(axis)
        up = [(i, i + 1) for i in range(count - 1)]
        down = [(j, i) for i, j in up]
        out.append(lax.ppermute(up_part, axis, up))
        out.append(lax.ppermute(down_part, axis, down))
    return out


def neighbour_of(t, d, sx, sy, sz):
    a, b, c = tile_coords(t, sy, sz)
    per_x = sy * sz
    table = (
        (a > 0, t - per_x),
        (a < sx - 1, t + per_x),
        (b > 0, t - sz),
        (b < sy - 1, t + sz),
        (c > 0, t - 1),
        (c < sz - 1, t + 1),
    )
    inside, nb = table[d]
    return inside, jnp.clip(nb, 0, sx * sy * sz - 1)


def make_step_kernel(sx, sy, sz, with_message):
    def kernel(*refs):
        face_refs = refs[:6]
        hxm_ref, hxp_ref, hym_ref, hyp_ref, coup_ref, phi_ref, plo_ref, landed_ref, inv_ref = refs[6:15]
        rest = refs[15:]
        if with_message:
            sel_ref, pthi_ref, ptlo_ref, out_ref, msg_ref, of_ref = rest[:6]
            side_refs = rest[6:10]
            faces_ref, acc_ref = rest[10:]
        else:
            out_ref, faces_ref = rest
        t = pl.program_id(0)
        a, b, c = tile_coords(t, sy, sz)
        zero = jnp.zeros((48, faces_ref.shape[-1]), BF16)
        halos = (
            (hxm_ref, b * sz + c),
            (hxp_ref, b * sz + c),
            (hym_ref, a * sz + c),
            (hyp_ref, a * sz + c),
            (None, None),
            (None, None),
        )
        for d in range(6):
            inside, _ = neighbour_of(t, d, sx, sy, sz)
            halo, slot = halos[d]
            src = face_refs[d]

            @pl.when(inside)
            def _():
                faces_ref[pl.ds(48 * d, 48), :] = src[0, 0]

            @pl.when(jnp.logical_not(inside))
            def _():
                faces_ref[pl.ds(48 * d, 48), :] = zero if halo is None else halo[slot]

        flux = jnp.dot(coup_ref[0], faces_ref[...], preferred_element_type=F32)
        landed = landed_ref[...]
        added = jnp.dot(phi_ref[0], landed, preferred_element_type=F32)
        added = added + jnp.dot(plo_ref[0], landed, preferred_element_type=F32)
        source = (flux + added).astype(BF16)
        new = (-jnp.dot(inv_ref[0], source, preferred_element_type=F32)).astype(BF16)
        out_ref[0] = new
        if with_message:
            faces_new = jnp.dot(sel_ref[...], new, preferred_element_type=F32).astype(BF16)
            of_ref[0] = faces_new
            emit_halos(faces_new, a, b, c, sx, sy, sz, side_refs)
            part = jnp.dot(pthi_ref[0], new, preferred_element_type=F32)
            part = part + jnp.dot(ptlo_ref[0], new, preferred_element_type=F32)

            @pl.when(t == 0)
            def _():
                acc_ref[...] = part

            @pl.when(t > 0)
            def _():
                acc_ref[...] += part

            @pl.when(t == pl.num_programs(0) - 1)
            def _():
                msg_ref[...] = acc_ref[...].astype(BF16)

    return kernel


def step_call(shape, faces, halos, coup, sel, p_hi, p_lo, landed, inv, pt_hi, pt_lo, with_message):
    sx, sy, sz, rows, cols = shape
    tiles = sx * sy * sz
    slots = landed.shape[0]
    faces4 = faces.reshape(tiles, 6, 48, cols)
    full3 = lambda shape: pl.BlockSpec(shape, lambda t: (0, 0, 0))
    full2 = lambda shape: pl.BlockSpec(shape, lambda t: (0, 0))
    tile3 = lambda shape: pl.BlockSpec((1,) + shape, lambda t: (t, 0, 0))

    def face_spec(d):
        return pl.BlockSpec((1, 1, 48, cols), lambda t: (neighbour_of(t, d, sx, sy, sz)[1], d, 0, 0))

    in_specs = [face_spec(d) for d in range(6)] + [
        full3(halos[0].shape),
        full3(halos[1].shape),
        full3(halos[2].shape),
        full3(halos[3].shape),
        tile3(coup.shape[1:]),
        tile3(p_hi.shape[1:]),
        tile3(p_lo.shape[1:]),
        full2(landed.shape),
        tile3(inv.shape[1:]),
    ]
    operands = [faces4] * 6 + [*halos, coup, p_hi, p_lo, landed, inv]
    out_shape = [jax.ShapeDtypeStruct((tiles, rows, cols), BF16)]
    out_specs = [tile3((rows, cols))]
    scratch = [pltpu.VMEM((6 * 48, cols), BF16)]
    if with_message:
        in_specs += [full2(sel.shape), tile3(pt_hi.shape[1:]), tile3(pt_lo.shape[1:])]
        operands += [sel, pt_hi, pt_lo]
        out_shape.append(jax.ShapeDtypeStruct((slots, cols), BF16))
        out_specs.append(full2((slots, cols)))
        shapes, specs = face_outputs(sx, sy, sz, cols)
        out_shape += shapes
        out_specs += specs
        scratch.append(pltpu.VMEM((slots, cols), F32))
    result = pl.pallas_call(
        make_step_kernel(sx, sy, sz, with_message),
        grid=(tiles,),
        in_specs=in_specs,
        out_specs=out_specs,
        out_shape=out_shape,
        scratch_shapes=scratch,
        compiler_params=pltpu.CompilerParams(
            dimension_semantics=("arbitrary",), vmem_limit_bytes=48 * 1024 * 1024
        ),
    )(*operands)
    new = result[0].reshape(shape)
    if not with_message:
        return new, None, None, None
    return new, result[1], result[2], list(result[3:7])


def exchange(values):
    return lax.all_to_all(values, ("gx", "gy"), split_axis=0, concat_axis=0, tiled=True)


def split(values):
    hi = values.astype(BF16)
    lo = (values - hi.astype(F32)).astype(BF16)
    return hi, lo


def local(
    later_adjoint,
    coupling,
    inverse_diag,
    tile_mask,
    perf_cell,
    perf_slot,
    perf_live,
    perf_coef,
    well_gain,
    misfit,
):
    sx, sy, sz, rows, cols = later_adjoint.shape
    tiles = sx * sy * sz
    slot_count = perf_cell.shape[1]
    peers = slot_count // CAPACITY
    wells_here = well_gain.shape[0]
    axes = ("gx", "gy")

    mask = tile_mask.astype(BF16).reshape(tiles, 6)
    coup = coupling.reshape(tiles, 6, rows, 48) * mask[:, :, None, None]
    coup = coup.transpose(0, 2, 1, 3).reshape(tiles, rows, 6 * 48)
    inv = inverse_diag.reshape(tiles, rows, rows)
    sel = jnp.asarray(selection().reshape(288, 192), BF16)

    in_use = perf_live[0].astype(F32)
    cell_ids = perf_cell[0]
    tile_of = cell_ids // 64
    cell_of = cell_ids % 64
    weights = [perf_coef[component, 0] * in_use for component in range(3)]

    def placement(slot_last):
        tile_ids = jnp.arange(tiles, dtype=jnp.int32)[:, None, None]
        if slot_last:
            unk_ids = jnp.arange(rows, dtype=jnp.int32)[None, :, None]
            pick = lambda v: v[None, None, :]
        else:
            unk_ids = jnp.arange(rows, dtype=jnp.int32)[None, None, :]
            pick = lambda v: v[None, :, None]
        place = 0.0
        for component in range(3):
            hit = (tile_ids == pick(tile_of)) & (unk_ids == pick(component * 64 + cell_of))
            place = place + jnp.where(hit, pick(weights[component]), 0.0)
        return split(place)

    p_hi, p_lo = placement(True)
    pt_hi, pt_lo = placement(False)

    slot_tag = perf_slot[0].astype(BF16).reshape(peers, CAPACITY, 1)
    well_index = jnp.arange(wells_here, dtype=jnp.int32).astype(BF16)

    adjoint = later_adjoint
    faces, sides = all_faces(later_adjoint, sel)
    flat0 = later_adjoint.reshape(tiles, rows, cols)
    message = (
        jnp.einsum("tup,tuc->pc", p_hi, flat0, preferred_element_type=F32)
        + jnp.einsum("tup,tuc->pc", p_lo, flat0, preferred_element_type=F32)
    ).astype(BF16)
    collected = []
    for sweep_index in range(STEPS):
        halos = send_faces(sides)
        payload = message.reshape(peers, CAPACITY, cols)
        if sweep_index == 0:
            tags = jnp.broadcast_to(slot_tag, (peers, CAPACITY, 128))
            payload = jnp.concatenate([payload, tags], axis=2)
        arrived = exchange(payload)
        if sweep_index == 0:
            arrived_tags = arrived[:, :, cols]
            selector = (arrived_tags.reshape(1, slot_count) == well_index[:, None]).astype(BF16)
        arrived = arrived[:, :, :cols]
        summed = jnp.dot(selector, arrived.reshape(slot_count, cols), preferred_element_type=F32)
        well_adj = (well_gain[:, None] * (summed + misfit[sweep_index])).astype(BF16)
        returned = jnp.einsum("ws,wr->sr", selector, well_adj, preferred_element_type=F32).astype(BF16)
        landed = exchange(returned.reshape(peers, CAPACITY, cols)).reshape(slot_count, cols)
        last = sweep_index == STEPS - 1
        adjoint, message, faces, sides = step_call(
            later_adjoint.shape, faces, halos, coup, sel, p_hi, p_lo, landed, inv, pt_hi, pt_lo, not last
        )
        collected.append(well_adj)
    return (adjoint, jnp.stack(collected))


def solution(mesh):
    return jax.shard_map(
        local,
        mesh=mesh,
        in_specs=(
            P("gx", "gy", None, None, None),
            P("gx", "gy", None, None, None, None),
            P("gx", "gy", None, None, None),
            P("gx", "gy", None, None),
            P(("gx", "gy"), None),
            P(("gx", "gy"), None),
            P(("gx", "gy"), None),
            P(None, ("gx", "gy"), None),
            P(("gx", "gy")),
            P(None, ("gx", "gy"), None),
        ),
        out_specs=(P("gx", "gy", None, None, None), P(None, ("gx", "gy"), None)),
        check_vma=False,
    )
```

```python
import numpy as np
import jax
import jax.numpy as jnp
from jax import lax
from jax.experimental import pallas as pl
from jax.experimental.pallas import tpu as pltpu
from jax.sharding import PartitionSpec as P


CAPACITY = 2
STEPS = 2
F32 = jnp.float32
BF16 = jnp.bfloat16


def face_rows():
    rows = np.zeros((6, 48), np.int32)
    for k in range(3):
        for p in range(4):
            for q in range(4):
                f = 16 * k + 4 * p + q
                rows[0, f] = 64 * k + 16 * 3 + 4 * p + q
                rows[1, f] = 64 * k + 4 * p + q
                rows[2, f] = 64 * k + 16 * p + 4 * 3 + q
                rows[3, f] = 64 * k + 16 * p + q
                rows[4, f] = 64 * k + 16 * p + 4 * q + 3
                rows[5, f] = 64 * k + 16 * p + 4 * q
    return rows


FACE_ROWS = face_rows()


def selection():
    sel = np.zeros((6, 48, 192), np.float32)
    for d in range(6):
        sel[d, np.arange(48), FACE_ROWS[d]] = 1.0
    return sel


def tile_coords(t, sy, sz):
    return t // (sy * sz), (t // sz) % sy, t % sz


def emit_halos(faces, a, b, c, sx, sy, sz, refs):
    ux_ref, dx_ref, uy_ref, dy_ref = refs
    cases = (
        (a == sx - 1, ux_ref, b * sz + c, 0),
        (a == 0, dx_ref, b * sz + c, 1),
        (b == sy - 1, uy_ref, a * sz + c, 2),
        (b == 0, dy_ref, a * sz + c, 3),
    )
    for on_side, ref, slot, d in cases:

        @pl.when(on_side)
        def _():
            ref[slot] = faces[48 * d : 48 * d + 48]


def face_outputs(sx, sy, sz, cols):
    tiles = sx * sy * sz
    shapes = [(sy * sz, 48, cols), (sy * sz, 48, cols), (sx * sz, 48, cols), (sx * sz, 48, cols)]
    specs = [pl.BlockSpec(shape, lambda t: (0, 0, 0)) for shape in shapes]
    out_shape = [jax.ShapeDtypeStruct((tiles, 288, cols), BF16)]
    out_specs = [pl.BlockSpec((1, 288, cols), lambda t: (t, 0, 0))]
    out_shape += [jax.ShapeDtypeStruct(shape, BF16) for shape in shapes]
    return out_shape, out_specs + specs


def faces_kernel(sx, sy, sz):
    def kernel(a_ref, sel_ref, of_ref, *refs):
        t = pl.program_id(0)
        a, b, c = tile_coords(t, sy, sz)
        faces = jnp.dot(sel_ref[...], a_ref[0], preferred_element_type=F32).astype(BF16)
        of_ref[0] = faces
        emit_halos(faces, a, b, c, sx, sy, sz, refs)

    return kernel


def all_faces(adjoint, sel):
    sx, sy, sz, rows, cols = adjoint.shape
    tiles = sx * sy * sz
    out_shape, out_specs = face_outputs(sx, sy, sz, cols)
    result = pl.pallas_call(
        faces_kernel(sx, sy, sz),
        grid=(tiles,),
        in_specs=[pl.BlockSpec((1, rows, cols), lambda t: (t, 0, 0)), pl.BlockSpec(sel.shape, lambda t: (0, 0))],
        out_specs=out_specs,
        out_shape=out_shape,
        compiler_params=pltpu.CompilerParams(dimension_semantics=("arbitrary",)),
    )(adjoint.reshape(tiles, rows, cols), sel)
    return result[0], list(result[1:])


def send_faces(sides):
    out = []
    for axis, up_part, down_part in (("gx", sides[0], sides[1]), ("gy", sides[2], sides[3])):
        count = lax.axis_size(axis)
        up = [(i, i + 1) for i in range(count - 1)]
        down = [(j, i) for i, j in up]
        out.append(lax.ppermute(up_part, axis, up))
        out.append(lax.ppermute(down_part, axis, down))
    return out


def neighbour_of(t, d, sx, sy, sz):
    a, b, c = tile_coords(t, sy, sz)
    per_x = sy * sz
    table = (
        (a > 0, t - per_x),
        (a < sx - 1, t + per_x),
        (b > 0, t - sz),
        (b < sy - 1, t + sz),
        (c > 0, t - 1),
        (c < sz - 1, t + 1),
    )
    inside, nb = table[d]
    return inside, jnp.clip(nb, 0, sx * sy * sz - 1)


def make_step_kernel(sx, sy, sz, with_message):
    def kernel(*refs):
        face_refs = refs[:6]
        hxm_ref, hxp_ref, hym_ref, hyp_ref, coup_ref, phi_ref, plo_ref, landed_ref, inv_ref = refs[6:15]
        rest = refs[15:]
        if with_message:
            sel_ref, pthi_ref, ptlo_ref, out_ref, msg_ref, of_ref = rest[:6]
            side_refs = rest[6:10]
            faces_ref, acc_ref = rest[10:]
        else:
            out_ref, faces_ref = rest
        t = pl.program_id(0)
        a, b, c = tile_coords(t, sy, sz)
        zero = jnp.zeros((48, faces_ref.shape[-1]), BF16)
        halos = (
            (hxm_ref, b * sz + c),
            (hxp_ref, b * sz + c),
            (hym_ref, a * sz + c),
            (hyp_ref, a * sz + c),
            (None, None),
            (None, None),
        )
        for d in range(6):
            inside, _ = neighbour_of(t, d, sx, sy, sz)
            halo, slot = halos[d]
            src = face_refs[d]

            @pl.when(inside)
            def _():
                faces_ref[pl.ds(48 * d, 48), :] = src[0, 0]

            @pl.when(jnp.logical_not(inside))
            def _():
                faces_ref[pl.ds(48 * d, 48), :] = zero if halo is None else halo[slot]

        flux = jnp.dot(coup_ref[0], faces_ref[...], preferred_element_type=F32)
        landed = landed_ref[...]
        added = jnp.dot(phi_ref[0], landed, preferred_element_type=F32)
        added = added + jnp.dot(plo_ref[0], landed, preferred_element_type=F32)
        source = (flux + added).astype(BF16)
        new = (-jnp.dot(inv_ref[0], source, preferred_element_type=F32)).astype(BF16)
        out_ref[0] = new
        if with_message:
            faces_new = jnp.dot(sel_ref[...], new, preferred_element_type=F32).astype(BF16)
            of_ref[0] = faces_new
            emit_halos(faces_new, a, b, c, sx, sy, sz, side_refs)
            part = jnp.dot(pthi_ref[0], new, preferred_element_type=F32)
            part = part + jnp.dot(ptlo_ref[0], new, preferred_element_type=F32)

            @pl.when(t == 0)
            def _():
                acc_ref[...] = part

            @pl.when(t > 0)
            def _():
                acc_ref[...] += part

            @pl.when(t == pl.num_programs(0) - 1)
            def _():
                msg_ref[...] = acc_ref[...].astype(BF16)

    return kernel


def step_call(shape, faces, halos, coup, sel, p_hi, p_lo, landed, inv, pt_hi, pt_lo, with_message):
    sx, sy, sz, rows, cols = shape
    tiles = sx * sy * sz
    slots = landed.shape[0]
    faces4 = faces.reshape(tiles, 6, 48, cols)
    full3 = lambda shape: pl.BlockSpec(shape, lambda t: (0, 0, 0))
    full2 = lambda shape: pl.BlockSpec(shape, lambda t: (0, 0))
    tile3 = lambda shape: pl.BlockSpec((1,) + shape, lambda t: (t, 0, 0))

    def face_spec(d):
        return pl.BlockSpec((1, 1, 48, cols), lambda t: (neighbour_of(t, d, sx, sy, sz)[1], d, 0, 0))

    in_specs = [face_spec(d) for d in range(6)] + [
        full3(halos[0].shape),
        full3(halos[1].shape),
        full3(halos[2].shape),
        full3(halos[3].shape),
        tile3(coup.shape[1:]),
        tile3(p_hi.shape[1:]),
        tile3(p_lo.shape[1:]),
        full2(landed.shape),
        tile3(inv.shape[1:]),
    ]
    operands = [faces4] * 6 + [*halos, coup, p_hi, p_lo, landed, inv]
    out_shape = [jax.ShapeDtypeStruct((tiles, rows, cols), BF16)]
    out_specs = [tile3((rows, cols))]
    scratch = [pltpu.VMEM((6 * 48, cols), BF16)]
    if with_message:
        in_specs += [full2(sel.shape), tile3(pt_hi.shape[1:]), tile3(pt_lo.shape[1:])]
        operands += [sel, pt_hi, pt_lo]
        out_shape.append(jax.ShapeDtypeStruct((slots, cols), BF16))
        out_specs.append(full2((slots, cols)))
        shapes, specs = face_outputs(sx, sy, sz, cols)
        out_shape += shapes
        out_specs += specs
        scratch.append(pltpu.VMEM((slots, cols), F32))
    result = pl.pallas_call(
        make_step_kernel(sx, sy, sz, with_message),
        grid=(tiles,),
        in_specs=in_specs,
        out_specs=out_specs,
        out_shape=out_shape,
        scratch_shapes=scratch,
        compiler_params=pltpu.CompilerParams(
            dimension_semantics=("arbitrary",), vmem_limit_bytes=48 * 1024 * 1024
        ),
    )(*operands)
    new = result[0].reshape(shape)
    if not with_message:
        return new, None, None, None
    return new, result[1], result[2], list(result[3:7])


def exchange(values):
    return lax.all_to_all(values, ("gx", "gy"), split_axis=0, concat_axis=0, tiled=True)


def split(values):
    hi = values.astype(BF16)
    lo = (values - hi.astype(F32)).astype(BF16)
    return hi, lo


def local(
    later_adjoint,
    coupling,
    inverse_diag,
    tile_mask,
    perf_cell,
    perf_slot,
    perf_live,
    perf_coef,
    well_gain,
    misfit,
):
    sx, sy, sz, rows, cols = later_adjoint.shape
    tiles = sx * sy * sz
    slot_count = perf_cell.shape[1]
    peers = slot_count // CAPACITY
    wells_here = well_gain.shape[0]
    axes = ("gx", "gy")

    mask = tile_mask.astype(BF16).reshape(tiles, 6)
    coup = coupling.reshape(tiles, 6, rows, 48) * mask[:, :, None, None]
    coup = coup.transpose(0, 2, 1, 3).reshape(tiles, rows, 6 * 48)
    inv = inverse_diag.reshape(tiles, rows, rows)
    sel = jnp.asarray(selection().reshape(288, 192), BF16)

    in_use = perf_live[0].astype(F32)
    cell_ids = perf_cell[0]
    tile_of = cell_ids // 64
    cell_of = cell_ids % 64
    weights = [perf_coef[component, 0] * in_use for component in range(3)]

    def placement(slot_last):
        tile_ids = jnp.arange(tiles, dtype=jnp.int32)[:, None, None]
        if slot_last:
            unk_ids = jnp.arange(rows, dtype=jnp.int32)[None, :, None]
            pick = lambda v: v[None, None, :]
        else:
            unk_ids = jnp.arange(rows, dtype=jnp.int32)[None, None, :]
            pick = lambda v: v[None, :, None]
        place = 0.0
        for component in range(3):
            hit = (tile_ids == pick(tile_of)) & (unk_ids == pick(component * 64 + cell_of))
            place = place + jnp.where(hit, pick(weights[component]), 0.0)
        return split(place)

    p_hi, p_lo = placement(True)
    pt_hi, pt_lo = placement(False)

    slot_tag = perf_slot[0].astype(BF16).reshape(peers, CAPACITY, 1)
    owners = jnp.arange(slot_count, dtype=jnp.int32) // CAPACITY
    well_ids = owners * wells_here + perf_slot[0]
    well_index = jnp.arange(wells_here, dtype=jnp.int32).astype(BF16)

    adjoint = later_adjoint
    faces, sides = all_faces(later_adjoint, sel)
    flat0 = later_adjoint.reshape(tiles, rows, cols)
    message = (
        jnp.einsum("tup,tuc->pc", p_hi, flat0, preferred_element_type=F32)
        + jnp.einsum("tup,tuc->pc", p_lo, flat0, preferred_element_type=F32)
    ).astype(BF16)
    collected = []
    for sweep_index in range(STEPS):
        halos = send_faces(sides)
        payload = message.reshape(peers, CAPACITY, cols)
        if sweep_index == 0:
            tags = jnp.broadcast_to(slot_tag, (peers, CAPACITY, 128))
            payload = jnp.concatenate([payload, tags], axis=2)
        arrived = exchange(payload)
        if sweep_index == 0:
            arrived_tags = arrived[:, :, cols]
            selector = (arrived_tags.reshape(1, slot_count) == well_index[:, None]).astype(BF16)
        arrived = arrived[:, :, :cols]
        summed = jnp.dot(selector, arrived.reshape(slot_count, cols), preferred_element_type=F32)
        well_adj = (well_gain[:, None] * (summed + misfit[sweep_index])).astype(BF16)
        gathered = lax.all_gather(well_adj, axes, axis=0, tiled=True)
        landed = jnp.take(gathered, well_ids, axis=0)
        last = sweep_index == STEPS - 1
        adjoint, message, faces, sides = step_call(
            later_adjoint.shape, faces, halos, coup, sel, p_hi, p_lo, landed, inv, pt_hi, pt_lo, not last
        )
        collected.append(well_adj)
    return (adjoint, jnp.stack(collected))


def solution(mesh):
    return jax.shard_map(
        local,
        mesh=mesh,
        in_specs=(
            P("gx", "gy", None, None, None),
            P("gx", "gy", None, None, None, None),
            P("gx", "gy", None, None, None),
            P("gx", "gy", None, None),
            P(("gx", "gy"), None),
            P(("gx", "gy"), None),
            P(("gx", "gy"), None),
            P(None, ("gx", "gy"), None),
            P(("gx", "gy")),
            P(None, ("gx", "gy"), None),
        ),
        out_specs=(P("gx", "gy", None, None, None), P(None, ("gx", "gy"), None)),
        check_vma=False,
    )
```

```python
import numpy as np
import jax
import jax.numpy as jnp
from jax import lax
from jax.experimental import pallas as pl
from jax.experimental.pallas import tpu as pltpu
from jax.sharding import PartitionSpec as P


CAPACITY = 2
STEPS = 2
F32 = jnp.float32
BF16 = jnp.bfloat16


def face_rows():
    rows = np.zeros((6, 48), np.int32)
    for k in range(3):
        for p in range(4):
            for q in range(4):
                f = 16 * k + 4 * p + q
                rows[0, f] = 64 * k + 16 * 3 + 4 * p + q
                rows[1, f] = 64 * k + 4 * p + q
                rows[2, f] = 64 * k + 16 * p + 4 * 3 + q
                rows[3, f] = 64 * k + 16 * p + q
                rows[4, f] = 64 * k + 16 * p + 4 * q + 3
                rows[5, f] = 64 * k + 16 * p + 4 * q
    return rows


FACE_ROWS = face_rows()


def selection():
    sel = np.zeros((6, 48, 192), np.float32)
    for d in range(6):
        sel[d, np.arange(48), FACE_ROWS[d]] = 1.0
    return sel


def tile_coords(t, sy, sz):
    return t // (sy * sz), (t // sz) % sy, t % sz


def emit_halos(faces, a, b, c, sx, sy, sz, refs):
    ux_ref, dx_ref, uy_ref, dy_ref = refs
    cases = (
        (a == sx - 1, ux_ref, b * sz + c, 0),
        (a == 0, dx_ref, b * sz + c, 1),
        (b == sy - 1, uy_ref, a * sz + c, 2),
        (b == 0, dy_ref, a * sz + c, 3),
    )
    for on_side, ref, slot, d in cases:

        @pl.when(on_side)
        def _():
            ref[slot] = faces[48 * d : 48 * d + 48]


def face_outputs(sx, sy, sz, cols):
    tiles = sx * sy * sz
    shapes = [(sy * sz, 48, cols), (sy * sz, 48, cols), (sx * sz, 48, cols), (sx * sz, 48, cols)]
    specs = [pl.BlockSpec(shape, lambda t: (0, 0, 0)) for shape in shapes]
    out_shape = [jax.ShapeDtypeStruct((tiles, 288, cols), BF16)]
    out_specs = [pl.BlockSpec((1, 288, cols), lambda t: (t, 0, 0))]
    out_shape += [jax.ShapeDtypeStruct(shape, BF16) for shape in shapes]
    return out_shape, out_specs + specs


def faces_kernel(sx, sy, sz):
    def kernel(a_ref, sel_ref, of_ref, *refs):
        t = pl.program_id(0)
        a, b, c = tile_coords(t, sy, sz)
        faces = jnp.dot(sel_ref[...], a_ref[0], preferred_element_type=F32).astype(BF16)
        of_ref[0] = faces
        emit_halos(faces, a, b, c, sx, sy, sz, refs)

    return kernel


def all_faces(adjoint, sel):
    sx, sy, sz, rows, cols = adjoint.shape
    tiles = sx * sy * sz
    out_shape, out_specs = face_outputs(sx, sy, sz, cols)
    result = pl.pallas_call(
        faces_kernel(sx, sy, sz),
        grid=(tiles,),
        in_specs=[pl.BlockSpec((1, rows, cols), lambda t: (t, 0, 0)), pl.BlockSpec(sel.shape, lambda t: (0, 0))],
        out_specs=out_specs,
        out_shape=out_shape,
        compiler_params=pltpu.CompilerParams(dimension_semantics=("arbitrary",)),
    )(adjoint.reshape(tiles, rows, cols), sel)
    return result[0], list(result[1:])


def send_faces(sides):
    out = []
    for axis, up_part, down_part in (("gx", sides[0], sides[1]), ("gy", sides[2], sides[3])):
        count = lax.axis_size(axis)
        up = [(i, i + 1) for i in range(count - 1)]
        down = [(j, i) for i, j in up]
        out.append(lax.ppermute(up_part, axis, up))
        out.append(lax.ppermute(down_part, axis, down))
    return out


def neighbour_of(t, d, sx, sy, sz):
    a, b, c = tile_coords(t, sy, sz)
    per_x = sy * sz
    table = (
        (a > 0, t - per_x),
        (a < sx - 1, t + per_x),
        (b > 0, t - sz),
        (b < sy - 1, t + sz),
        (c > 0, t - 1),
        (c < sz - 1, t + 1),
    )
    inside, nb = table[d]
    return inside, jnp.clip(nb, 0, sx * sy * sz - 1)


def make_step_kernel(sx, sy, sz, with_message):
    def kernel(*refs):
        face_refs = refs[:6]
        hxm_ref, hxp_ref, hym_ref, hyp_ref, coup_ref, phi_ref, plo_ref, landed_ref, inv_ref = refs[6:15]
        rest = refs[15:]
        if with_message:
            sel_ref, pthi_ref, ptlo_ref, out_ref, msg_ref, of_ref = rest[:6]
            side_refs = rest[6:10]
            faces_ref, added_ref, acc_ref = rest[10:]
        else:
            out_ref, faces_ref, added_ref = rest
        t = pl.program_id(0)
        a, b, c = tile_coords(t, sy, sz)
        zero = jnp.zeros((48, faces_ref.shape[-1]), BF16)
        halos = (
            (hxm_ref, b * sz + c),
            (hxp_ref, b * sz + c),
            (hym_ref, a * sz + c),
            (hyp_ref, a * sz + c),
            (None, None),
            (None, None),
        )
        for d in range(6):
            inside, _ = neighbour_of(t, d, sx, sy, sz)
            halo, slot = halos[d]
            src = face_refs[d]

            @pl.when(inside)
            def _():
                faces_ref[pl.ds(48 * d, 48), :] = src[0, 0]

            @pl.when(jnp.logical_not(inside))
            def _():
                faces_ref[pl.ds(48 * d, 48), :] = zero if halo is None else halo[slot]

        @pl.when(t == 0)
        def _():
            landed = landed_ref[...]
            whole = jnp.dot(phi_ref[...], landed, preferred_element_type=F32)
            added_ref[...] = whole + jnp.dot(plo_ref[...], landed, preferred_element_type=F32)

        rows = coup_ref.shape[1]
        flux = jnp.dot(coup_ref[0], faces_ref[...], preferred_element_type=F32)
        added = added_ref[pl.ds(pl.multiple_of(t * rows, 8), rows), :]
        source = (flux + added).astype(BF16)
        new = (-jnp.dot(inv_ref[0], source, preferred_element_type=F32)).astype(BF16)
        out_ref[0] = new
        if with_message:
            faces_new = jnp.dot(sel_ref[...], new, preferred_element_type=F32).astype(BF16)
            of_ref[0] = faces_new
            emit_halos(faces_new, a, b, c, sx, sy, sz, side_refs)
            part = jnp.dot(pthi_ref[0], new, preferred_element_type=F32)
            part = part + jnp.dot(ptlo_ref[0], new, preferred_element_type=F32)

            @pl.when(t == 0)
            def _():
                acc_ref[...] = part

            @pl.when(t > 0)
            def _():
                acc_ref[...] += part

            @pl.when(t == pl.num_programs(0) - 1)
            def _():
                msg_ref[...] = acc_ref[...].astype(BF16)

    return kernel


def step_call(shape, faces, halos, coup, sel, p_hi, p_lo, landed, inv, pt_hi, pt_lo, with_message):
    sx, sy, sz, rows, cols = shape
    tiles = sx * sy * sz
    slots = landed.shape[0]
    faces4 = faces.reshape(tiles, 6, 48, cols)
    full3 = lambda shape: pl.BlockSpec(shape, lambda t: (0, 0, 0))
    full2 = lambda shape: pl.BlockSpec(shape, lambda t: (0, 0))
    tile3 = lambda shape: pl.BlockSpec((1,) + shape, lambda t: (t, 0, 0))

    def face_spec(d):
        return pl.BlockSpec((1, 1, 48, cols), lambda t: (neighbour_of(t, d, sx, sy, sz)[1], d, 0, 0))

    in_specs = [face_spec(d) for d in range(6)] + [
        full3(halos[0].shape),
        full3(halos[1].shape),
        full3(halos[2].shape),
        full3(halos[3].shape),
        tile3(coup.shape[1:]),
        full2((tiles * rows, slots)),
        full2((tiles * rows, slots)),
        full2(landed.shape),
        tile3(inv.shape[1:]),
    ]
    flat_hi = p_hi.reshape(tiles * rows, slots)
    flat_lo = p_lo.reshape(tiles * rows, slots)
    operands = [faces4] * 6 + [*halos, coup, flat_hi, flat_lo, landed, inv]
    out_shape = [jax.ShapeDtypeStruct((tiles, rows, cols), BF16)]
    out_specs = [tile3((rows, cols))]
    scratch = [pltpu.VMEM((6 * 48, cols), BF16), pltpu.VMEM((tiles * rows, cols), F32)]
    if with_message:
        in_specs += [full2(sel.shape), tile3(pt_hi.shape[1:]), tile3(pt_lo.shape[1:])]
        operands += [sel, pt_hi, pt_lo]
        out_shape.append(jax.ShapeDtypeStruct((slots, cols), BF16))
        out_specs.append(full2((slots, cols)))
        shapes, specs = face_outputs(sx, sy, sz, cols)
        out_shape += shapes
        out_specs += specs
        scratch.append(pltpu.VMEM((slots, cols), F32))
    result = pl.pallas_call(
        make_step_kernel(sx, sy, sz, with_message),
        grid=(tiles,),
        in_specs=in_specs,
        out_specs=out_specs,
        out_shape=out_shape,
        scratch_shapes=scratch,
        compiler_params=pltpu.CompilerParams(
            dimension_semantics=("arbitrary",), vmem_limit_bytes=56 * 1024 * 1024
        ),
    )(*operands)
    new = result[0].reshape(shape)
    if not with_message:
        return new, None, None, None
    return new, result[1], result[2], list(result[3:7])


def exchange(values):
    return lax.all_to_all(values, ("gx", "gy"), split_axis=0, concat_axis=0, tiled=True)


def split(values):
    hi = values.astype(BF16)
    lo = (values - hi.astype(F32)).astype(BF16)
    return hi, lo


def local(
    later_adjoint,
    coupling,
    inverse_diag,
    tile_mask,
    perf_cell,
    perf_slot,
    perf_live,
    perf_coef,
    well_gain,
    misfit,
):
    sx, sy, sz, rows, cols = later_adjoint.shape
    tiles = sx * sy * sz
    slot_count = perf_cell.shape[1]
    peers = slot_count // CAPACITY
    wells_here = well_gain.shape[0]
    axes = ("gx", "gy")

    mask = tile_mask.astype(BF16).reshape(tiles, 6)
    coup = coupling.reshape(tiles, 6, rows, 48) * mask[:, :, None, None]
    coup = coup.transpose(0, 2, 1, 3).reshape(tiles, rows, 6 * 48)
    inv = inverse_diag.reshape(tiles, rows, rows)
    sel = jnp.asarray(selection().reshape(288, 192), BF16)

    in_use = perf_live[0].astype(F32)
    cell_ids = perf_cell[0]
    tile_of = cell_ids // 64
    cell_of = cell_ids % 64
    weights = [perf_coef[component, 0] * in_use for component in range(3)]

    def placement(slot_last):
        tile_ids = jnp.arange(tiles, dtype=jnp.int32)[:, None, None]
        if slot_last:
            unk_ids = jnp.arange(rows, dtype=jnp.int32)[None, :, None]
            pick = lambda v: v[None, None, :]
        else:
            unk_ids = jnp.arange(rows, dtype=jnp.int32)[None, None, :]
            pick = lambda v: v[None, :, None]
        place = 0.0
        for component in range(3):
            hit = (tile_ids == pick(tile_of)) & (unk_ids == pick(component * 64 + cell_of))
            place = place + jnp.where(hit, pick(weights[component]), 0.0)
        return split(place)

    p_hi, p_lo = placement(True)
    pt_hi, pt_lo = placement(False)

    slot_tag = perf_slot[0].astype(BF16).reshape(peers, CAPACITY, 1)
    well_index = jnp.arange(wells_here, dtype=jnp.int32).astype(BF16)

    adjoint = later_adjoint
    faces, sides = all_faces(later_adjoint, sel)
    flat0 = later_adjoint.reshape(tiles, rows, cols)
    message = (
        jnp.einsum("tup,tuc->pc", p_hi, flat0, preferred_element_type=F32)
        + jnp.einsum("tup,tuc->pc", p_lo, flat0, preferred_element_type=F32)
    ).astype(BF16)
    collected = []
    for sweep_index in range(STEPS):
        halos = send_faces(sides)
        payload = message.reshape(peers, CAPACITY, cols)
        if sweep_index == 0:
            tags = jnp.broadcast_to(slot_tag, (peers, CAPACITY, 128))
            payload = jnp.concatenate([payload, tags], axis=2)
        arrived = exchange(payload)
        if sweep_index == 0:
            arrived_tags = arrived[:, :, cols]
            selector = (arrived_tags.reshape(1, slot_count) == well_index[:, None]).astype(BF16)
        arrived = arrived[:, :, :cols]
        summed = jnp.dot(selector, arrived.reshape(slot_count, cols), preferred_element_type=F32)
        well_adj = (well_gain[:, None] * (summed + misfit[sweep_index])).astype(BF16)
        returned = jnp.einsum("ws,wr->sr", selector, well_adj, preferred_element_type=F32).astype(BF16)
        landed = exchange(returned.reshape(peers, CAPACITY, cols)).reshape(slot_count, cols)
        last = sweep_index == STEPS - 1
        adjoint, message, faces, sides = step_call(
            later_adjoint.shape, faces, halos, coup, sel, p_hi, p_lo, landed, inv, pt_hi, pt_lo, not last
        )
        collected.append(well_adj)
    return (adjoint, jnp.stack(collected))


def solution(mesh):
    return jax.shard_map(
        local,
        mesh=mesh,
        in_specs=(
            P("gx", "gy", None, None, None),
            P("gx", "gy", None, None, None, None),
            P("gx", "gy", None, None, None),
            P("gx", "gy", None, None),
            P(("gx", "gy"), None),
            P(("gx", "gy"), None),
            P(("gx", "gy"), None),
            P(None, ("gx", "gy"), None),
            P(("gx", "gy")),
            P(None, ("gx", "gy"), None),
        ),
        out_specs=(P("gx", "gy", None, None, None), P(None, ("gx", "gy"), None)),
        check_vma=False,
    )
```

```python
import numpy as np
import jax
import jax.numpy as jnp
from jax import lax
from jax.experimental import pallas as pl
from jax.experimental.pallas import tpu as pltpu
from jax.sharding import PartitionSpec as P


CAPACITY = 2
STEPS = 2
F32 = jnp.float32
BF16 = jnp.bfloat16


def face_rows():
    rows = np.zeros((6, 48), np.int32)
    for k in range(3):
        for p in range(4):
            for q in range(4):
                f = 16 * k + 4 * p + q
                rows[0, f] = 64 * k + 16 * 3 + 4 * p + q
                rows[1, f] = 64 * k + 4 * p + q
                rows[2, f] = 64 * k + 16 * p + 4 * 3 + q
                rows[3, f] = 64 * k + 16 * p + q
                rows[4, f] = 64 * k + 16 * p + 4 * q + 3
                rows[5, f] = 64 * k + 16 * p + 4 * q
    return rows


FACE_ROWS = face_rows()


def selection():
    sel = np.zeros((6, 48, 192), np.float32)
    for d in range(6):
        sel[d, np.arange(48), FACE_ROWS[d]] = 1.0
    return sel


def tile_coords(t, sy, sz):
    return t // (sy * sz), (t // sz) % sy, t % sz


def emit_halos(faces, a, b, c, sx, sy, sz, refs):
    ux_ref, dx_ref, uy_ref, dy_ref = refs
    cases = (
        (a == sx - 1, ux_ref, b * sz + c, 0),
        (a == 0, dx_ref, b * sz + c, 1),
        (b == sy - 1, uy_ref, a * sz + c, 2),
        (b == 0, dy_ref, a * sz + c, 3),
    )
    for on_side, ref, slot, d in cases:

        @pl.when(on_side)
        def _():
            ref[slot] = faces[48 * d : 48 * d + 48]


def face_outputs(sx, sy, sz, cols):
    tiles = sx * sy * sz
    shapes = [(sy * sz, 48, cols), (sy * sz, 48, cols), (sx * sz, 48, cols), (sx * sz, 48, cols)]
    specs = [pl.BlockSpec(shape, lambda t: (0, 0, 0)) for shape in shapes]
    out_shape = [jax.ShapeDtypeStruct((tiles, 288, cols), BF16)]
    out_specs = [pl.BlockSpec((1, 288, cols), lambda t: (t, 0, 0))]
    out_shape += [jax.ShapeDtypeStruct(shape, BF16) for shape in shapes]
    return out_shape, out_specs + specs


def faces_kernel(sx, sy, sz):
    def kernel(a_ref, sel_ref, of_ref, *refs):
        t = pl.program_id(0)
        a, b, c = tile_coords(t, sy, sz)
        faces = jnp.dot(sel_ref[...], a_ref[0], preferred_element_type=F32).astype(BF16)
        of_ref[0] = faces
        emit_halos(faces, a, b, c, sx, sy, sz, refs)

    return kernel


def all_faces(adjoint, sel):
    sx, sy, sz, rows, cols = adjoint.shape
    tiles = sx * sy * sz
    out_shape, out_specs = face_outputs(sx, sy, sz, cols)
    result = pl.pallas_call(
        faces_kernel(sx, sy, sz),
        grid=(tiles,),
        in_specs=[pl.BlockSpec((1, rows, cols), lambda t: (t, 0, 0)), pl.BlockSpec(sel.shape, lambda t: (0, 0))],
        out_specs=out_specs,
        out_shape=out_shape,
        compiler_params=pltpu.CompilerParams(dimension_semantics=("arbitrary",)),
    )(adjoint.reshape(tiles, rows, cols), sel)
    return result[0], list(result[1:])


def send_faces(sides):
    out = []
    for axis, up_part, down_part in (("gx", sides[0], sides[1]), ("gy", sides[2], sides[3])):
        count = lax.axis_size(axis)
        up = [(i, i + 1) for i in range(count - 1)]
        down = [(j, i) for i, j in up]
        out.append(lax.ppermute(up_part, axis, up))
        out.append(lax.ppermute(down_part, axis, down))
    return out


def neighbour_of(t, d, sx, sy, sz):
    a, b, c = tile_coords(t, sy, sz)
    per_x = sy * sz
    table = (
        (a > 0, t - per_x),
        (a < sx - 1, t + per_x),
        (b > 0, t - sz),
        (b < sy - 1, t + sz),
        (c > 0, t - 1),
        (c < sz - 1, t + 1),
    )
    inside, nb = table[d]
    return inside, jnp.clip(nb, 0, sx * sy * sz - 1)


def make_step_kernel(sx, sy, sz, with_message):
    def kernel(*refs):
        face_refs = refs[:6]
        hxm_ref, hxp_ref, hym_ref, hyp_ref, coup_ref, phi_ref, plo_ref, landed_ref, inv_ref = refs[6:15]
        rest = refs[15:]
        if with_message:
            sel_ref, pthi_ref, ptlo_ref, out_ref, msg_ref, of_ref = rest[:6]
            side_refs = rest[6:10]
            faces_ref, added_ref, acc_ref = rest[10:]
        else:
            out_ref, faces_ref, added_ref = rest
        t = pl.program_id(0)
        a, b, c = tile_coords(t, sy, sz)
        zero = jnp.zeros((48, faces_ref.shape[-1]), BF16)
        halos = (
            (hxm_ref, b * sz + c),
            (hxp_ref, b * sz + c),
            (hym_ref, a * sz + c),
            (hyp_ref, a * sz + c),
            (None, None),
            (None, None),
        )
        for d in range(6):
            inside, _ = neighbour_of(t, d, sx, sy, sz)
            halo, slot = halos[d]
            src = face_refs[d]

            @pl.when(inside)
            def _():
                faces_ref[pl.ds(48 * d, 48), :] = src[0, 0]

            @pl.when(jnp.logical_not(inside))
            def _():
                faces_ref[pl.ds(48 * d, 48), :] = zero if halo is None else halo[slot]

        @pl.when(t == 0)
        def _():
            landed = landed_ref[...]
            whole = jnp.dot(phi_ref[...], landed, preferred_element_type=F32)
            added_ref[...] = whole + jnp.dot(plo_ref[...], landed, preferred_element_type=F32)

        rows = coup_ref.shape[1]
        flux = jnp.dot(coup_ref[0], faces_ref[...], preferred_element_type=F32)
        added = added_ref[pl.ds(pl.multiple_of(t * rows, 8), rows), :]
        source = (flux + added).astype(BF16)
        new = (-jnp.dot(inv_ref[0], source, preferred_element_type=F32)).astype(BF16)
        out_ref[0] = new
        if with_message:
            n_sel, n_slot = sel_ref.shape[0], pthi_ref.shape[1]
            lhs = jnp.concatenate([sel_ref[...], pthi_ref[0], ptlo_ref[0]], axis=0)
            both = jnp.dot(lhs, new, preferred_element_type=F32)
            faces_new = both[:n_sel].astype(BF16)
            of_ref[0] = faces_new
            emit_halos(faces_new, a, b, c, sx, sy, sz, side_refs)
            part = both[n_sel : n_sel + n_slot] + both[n_sel + n_slot :]

            @pl.when(t == 0)
            def _():
                acc_ref[...] = part

            @pl.when(t > 0)
            def _():
                acc_ref[...] += part

            @pl.when(t == pl.num_programs(0) - 1)
            def _():
                msg_ref[...] = acc_ref[...].astype(BF16)

    return kernel


def step_call(shape, faces, halos, coup, sel, p_hi, p_lo, landed, inv, pt_hi, pt_lo, with_message):
    sx, sy, sz, rows, cols = shape
    tiles = sx * sy * sz
    slots = landed.shape[0]
    faces4 = faces.reshape(tiles, 6, 48, cols)
    full3 = lambda shape: pl.BlockSpec(shape, lambda t: (0, 0, 0))
    full2 = lambda shape: pl.BlockSpec(shape, lambda t: (0, 0))
    tile3 = lambda shape: pl.BlockSpec((1,) + shape, lambda t: (t, 0, 0))

    def face_spec(d):
        return pl.BlockSpec((1, 1, 48, cols), lambda t: (neighbour_of(t, d, sx, sy, sz)[1], d, 0, 0))

    in_specs = [face_spec(d) for d in range(6)] + [
        full3(halos[0].shape),
        full3(halos[1].shape),
        full3(halos[2].shape),
        full3(halos[3].shape),
        tile3(coup.shape[1:]),
        full2((tiles * rows, slots)),
        full2((tiles * rows, slots)),
        full2(landed.shape),
        tile3(inv.shape[1:]),
    ]
    flat_hi = p_hi.reshape(tiles * rows, slots)
    flat_lo = p_lo.reshape(tiles * rows, slots)
    operands = [faces4] * 6 + [*halos, coup, flat_hi, flat_lo, landed, inv]
    out_shape = [jax.ShapeDtypeStruct((tiles, rows, cols), BF16)]
    out_specs = [tile3((rows, cols))]
    scratch = [pltpu.VMEM((6 * 48, cols), BF16), pltpu.VMEM((tiles * rows, cols), F32)]
    if with_message:
        in_specs += [full2(sel.shape), tile3(pt_hi.shape[1:]), tile3(pt_lo.shape[1:])]
        operands += [sel, pt_hi, pt_lo]
        out_shape.append(jax.ShapeDtypeStruct((slots, cols), BF16))
        out_specs.append(full2((slots, cols)))
        shapes, specs = face_outputs(sx, sy, sz, cols)
        out_shape += shapes
        out_specs += specs
        scratch.append(pltpu.VMEM((slots, cols), F32))
    result = pl.pallas_call(
        make_step_kernel(sx, sy, sz, with_message),
        grid=(tiles,),
        in_specs=in_specs,
        out_specs=out_specs,
        out_shape=out_shape,
        scratch_shapes=scratch,
        compiler_params=pltpu.CompilerParams(
            dimension_semantics=("arbitrary",), vmem_limit_bytes=56 * 1024 * 1024
        ),
    )(*operands)
    new = result[0].reshape(shape)
    if not with_message:
        return new, None, None, None
    return new, result[1], result[2], list(result[3:7])


def exchange(values):
    return lax.all_to_all(values, ("gx", "gy"), split_axis=0, concat_axis=0, tiled=True)


def split(values):
    hi = values.astype(BF16)
    lo = (values - hi.astype(F32)).astype(BF16)
    return hi, lo


def local(
    later_adjoint,
    coupling,
    inverse_diag,
    tile_mask,
    perf_cell,
    perf_slot,
    perf_live,
    perf_coef,
    well_gain,
    misfit,
):
    sx, sy, sz, rows, cols = later_adjoint.shape
    tiles = sx * sy * sz
    slot_count = perf_cell.shape[1]
    peers = slot_count // CAPACITY
    wells_here = well_gain.shape[0]
    axes = ("gx", "gy")

    mask = tile_mask.astype(BF16).reshape(tiles, 6)
    coup = coupling.reshape(tiles, 6, rows, 48) * mask[:, :, None, None]
    coup = coup.transpose(0, 2, 1, 3).reshape(tiles, rows, 6 * 48)
    inv = inverse_diag.reshape(tiles, rows, rows)
    sel = jnp.asarray(selection().reshape(288, 192), BF16)

    in_use = perf_live[0].astype(F32)
    cell_ids = perf_cell[0]
    tile_of = cell_ids // 64
    cell_of = cell_ids % 64
    weights = [perf_coef[component, 0] * in_use for component in range(3)]

    def placement(slot_last):
        tile_ids = jnp.arange(tiles, dtype=jnp.int32)[:, None, None]
        if slot_last:
            unk_ids = jnp.arange(rows, dtype=jnp.int32)[None, :, None]
            pick = lambda v: v[None, None, :]
        else:
            unk_ids = jnp.arange(rows, dtype=jnp.int32)[None, None, :]
            pick = lambda v: v[None, :, None]
        place = 0.0
        for component in range(3):
            hit = (tile_ids == pick(tile_of)) & (unk_ids == pick(component * 64 + cell_of))
            place = place + jnp.where(hit, pick(weights[component]), 0.0)
        return split(place)

    p_hi, p_lo = placement(True)
    pt_hi, pt_lo = placement(False)

    slot_tag = perf_slot[0].astype(BF16).reshape(peers, CAPACITY, 1)
    well_index = jnp.arange(wells_here, dtype=jnp.int32).astype(BF16)

    adjoint = later_adjoint
    faces, sides = all_faces(later_adjoint, sel)
    flat0 = later_adjoint.reshape(tiles, rows, cols)
    message = (
        jnp.einsum("tup,tuc->pc", p_hi, flat0, preferred_element_type=F32)
        + jnp.einsum("tup,tuc->pc", p_lo, flat0, preferred_element_type=F32)
    ).astype(BF16)
    collected = []
    for sweep_index in range(STEPS):
        halos = send_faces(sides)
        payload = message.reshape(peers, CAPACITY, cols)
        if sweep_index == 0:
            tags = jnp.broadcast_to(slot_tag, (peers, CAPACITY, 128))
            payload = jnp.concatenate([payload, tags], axis=2)
        arrived = exchange(payload)
        if sweep_index == 0:
            arrived_tags = arrived[:, :, cols]
            selector = (arrived_tags.reshape(1, slot_count) == well_index[:, None]).astype(BF16)
        arrived = arrived[:, :, :cols]
        summed = jnp.dot(selector, arrived.reshape(slot_count, cols), preferred_element_type=F32)
        well_adj = (well_gain[:, None] * (summed + misfit[sweep_index])).astype(BF16)
        returned = jnp.einsum("ws,wr->sr", selector, well_adj, preferred_element_type=F32).astype(BF16)
        landed = exchange(returned.reshape(peers, CAPACITY, cols)).reshape(slot_count, cols)
        last = sweep_index == STEPS - 1
        adjoint, message, faces, sides = step_call(
            later_adjoint.shape, faces, halos, coup, sel, p_hi, p_lo, landed, inv, pt_hi, pt_lo, not last
        )
        collected.append(well_adj)
    return (adjoint, jnp.stack(collected))


def solution(mesh):
    return jax.shard_map(
        local,
        mesh=mesh,
        in_specs=(
            P("gx", "gy", None, None, None),
            P("gx", "gy", None, None, None, None),
            P("gx", "gy", None, None, None),
            P("gx", "gy", None, None),
            P(("gx", "gy"), None),
            P(("gx", "gy"), None),
            P(("gx", "gy"), None),
            P(None, ("gx", "gy"), None),
            P(("gx", "gy")),
            P(None, ("gx", "gy"), None),
        ),
        out_specs=(P("gx", "gy", None, None, None), P(None, ("gx", "gy"), None)),
        check_vma=False,
    )
```

```python
import numpy as np
import jax
import jax.numpy as jnp
from jax import lax
from jax.experimental import pallas as pl
from jax.experimental.pallas import tpu as pltpu
from jax.sharding import PartitionSpec as P


CAPACITY = 2
STEPS = 2
F32 = jnp.float32
BF16 = jnp.bfloat16


def face_rows():
    rows = np.zeros((6, 48), np.int32)
    for k in range(3):
        for p in range(4):
            for q in range(4):
                f = 16 * k + 4 * p + q
                rows[0, f] = 64 * k + 16 * 3 + 4 * p + q
                rows[1, f] = 64 * k + 4 * p + q
                rows[2, f] = 64 * k + 16 * p + 4 * 3 + q
                rows[3, f] = 64 * k + 16 * p + q
                rows[4, f] = 64 * k + 16 * p + 4 * q + 3
                rows[5, f] = 64 * k + 16 * p + 4 * q
    return rows


FACE_ROWS = face_rows()


def selection():
    sel = np.zeros((6, 48, 192), np.float32)
    for d in range(6):
        sel[d, np.arange(48), FACE_ROWS[d]] = 1.0
    return sel


def tile_coords(t, sy, sz):
    return t // (sy * sz), (t // sz) % sy, t % sz


def emit_halos(faces, a, b, c, sx, sy, sz, refs):
    ux_ref, dx_ref, uy_ref, dy_ref = refs
    cases = (
        (a == sx - 1, ux_ref, b * sz + c, 0),
        (a == 0, dx_ref, b * sz + c, 1),
        (b == sy - 1, uy_ref, a * sz + c, 2),
        (b == 0, dy_ref, a * sz + c, 3),
    )
    for on_side, ref, slot, d in cases:

        @pl.when(on_side)
        def _():
            ref[slot] = faces[48 * d : 48 * d + 48]


def face_outputs(sx, sy, sz, cols):
    tiles = sx * sy * sz
    shapes = [(sy * sz, 48, cols), (sy * sz, 48, cols), (sx * sz, 48, cols), (sx * sz, 48, cols)]
    specs = [pl.BlockSpec(shape, lambda t: (0, 0, 0)) for shape in shapes]
    out_shape = [jax.ShapeDtypeStruct((tiles, 288, cols), BF16)]
    out_specs = [pl.BlockSpec((1, 288, cols), lambda t: (t, 0, 0))]
    out_shape += [jax.ShapeDtypeStruct(shape, BF16) for shape in shapes]
    return out_shape, out_specs + specs


def faces_kernel(sx, sy, sz):
    def kernel(a_ref, sel_ref, of_ref, *refs):
        t = pl.program_id(0)
        a, b, c = tile_coords(t, sy, sz)
        faces = jnp.dot(sel_ref[...], a_ref[0], preferred_element_type=F32).astype(BF16)
        of_ref[0] = faces
        emit_halos(faces, a, b, c, sx, sy, sz, refs)

    return kernel


def all_faces(adjoint, sel):
    sx, sy, sz, rows, cols = adjoint.shape
    tiles = sx * sy * sz
    out_shape, out_specs = face_outputs(sx, sy, sz, cols)
    result = pl.pallas_call(
        faces_kernel(sx, sy, sz),
        grid=(tiles,),
        in_specs=[pl.BlockSpec((1, rows, cols), lambda t: (t, 0, 0)), pl.BlockSpec(sel.shape, lambda t: (0, 0))],
        out_specs=out_specs,
        out_shape=out_shape,
        compiler_params=pltpu.CompilerParams(dimension_semantics=("arbitrary",)),
    )(adjoint.reshape(tiles, rows, cols), sel)
    return result[0], list(result[1:])


def send_faces(sides):
    out = []
    for axis, up_part, down_part in (("gx", sides[0], sides[1]), ("gy", sides[2], sides[3])):
        count = lax.axis_size(axis)
        up = [(i, i + 1) for i in range(count - 1)]
        down = [(j, i) for i, j in up]
        out.append(lax.ppermute(up_part, axis, up))
        out.append(lax.ppermute(down_part, axis, down))
    return out


def neighbour_of(t, d, sx, sy, sz):
    a, b, c = tile_coords(t, sy, sz)
    per_x = sy * sz
    table = (
        (a > 0, t - per_x),
        (a < sx - 1, t + per_x),
        (b > 0, t - sz),
        (b < sy - 1, t + sz),
        (c > 0, t - 1),
        (c < sz - 1, t + 1),
    )
    inside, nb = table[d]
    return inside, jnp.clip(nb, 0, sx * sy * sz - 1)


def make_step_kernel(sx, sy, sz, with_message):
    def kernel(*refs):
        face_refs = refs[:6]
        hxm_ref, hxp_ref, hym_ref, hyp_ref, coup_ref, phi_ref, plo_ref, landed_ref, inv_ref = refs[6:15]
        rest = refs[15:]
        if with_message:
            sel_ref, pthi_ref, ptlo_ref, out_ref, msg_ref, of_ref = rest[:6]
            side_refs = rest[6:10]
            faces_ref, acc_ref = rest[10:]
        else:
            out_ref, faces_ref = rest
        t = pl.program_id(0)
        a, b, c = tile_coords(t, sy, sz)
        zero = jnp.zeros((48, faces_ref.shape[-1]), BF16)
        halos = (
            (hxm_ref, b * sz + c),
            (hxp_ref, b * sz + c),
            (hym_ref, a * sz + c),
            (hyp_ref, a * sz + c),
            (None, None),
            (None, None),
        )
        for d in range(6):
            inside, _ = neighbour_of(t, d, sx, sy, sz)
            halo, slot = halos[d]
            src = face_refs[d]

            @pl.when(inside)
            def _():
                faces_ref[pl.ds(48 * d, 48), :] = src[0, 0]

            @pl.when(jnp.logical_not(inside))
            def _():
                faces_ref[pl.ds(48 * d, 48), :] = zero if halo is None else halo[slot]

        rows = coup_ref.shape[1]
        flux = jnp.dot(coup_ref[0], faces_ref[...], preferred_element_type=F32)
        both = jnp.dot(jnp.concatenate([phi_ref[0], plo_ref[0]], axis=0), landed_ref[...], preferred_element_type=F32)
        added = both[:rows] + both[rows:]
        source = (flux + added).astype(BF16)
        new = (-jnp.dot(inv_ref[0], source, preferred_element_type=F32)).astype(BF16)
        out_ref[0] = new
        if with_message:
            n_sel, n_slot = sel_ref.shape[0], pthi_ref.shape[1]
            lhs = jnp.concatenate([sel_ref[...], pthi_ref[0], ptlo_ref[0]], axis=0)
            both = jnp.dot(lhs, new, preferred_element_type=F32)
            faces_new = both[:n_sel].astype(BF16)
            of_ref[0] = faces_new
            emit_halos(faces_new, a, b, c, sx, sy, sz, side_refs)
            part = both[n_sel : n_sel + n_slot] + both[n_sel + n_slot :]

            @pl.when(t == 0)
            def _():
                acc_ref[...] = part

            @pl.when(t > 0)
            def _():
                acc_ref[...] += part

            @pl.when(t == pl.num_programs(0) - 1)
            def _():
                msg_ref[...] = acc_ref[...].astype(BF16)

    return kernel


def step_call(shape, faces, halos, coup, sel, p_hi, p_lo, landed, inv, pt_hi, pt_lo, with_message):
    sx, sy, sz, rows, cols = shape
    tiles = sx * sy * sz
    slots = landed.shape[0]
    faces4 = faces.reshape(tiles, 6, 48, cols)
    full3 = lambda shape: pl.BlockSpec(shape, lambda t: (0, 0, 0))
    full2 = lambda shape: pl.BlockSpec(shape, lambda t: (0, 0))
    tile3 = lambda shape: pl.BlockSpec((1,) + shape, lambda t: (t, 0, 0))

    def face_spec(d):
        return pl.BlockSpec((1, 1, 48, cols), lambda t: (neighbour_of(t, d, sx, sy, sz)[1], d, 0, 0))

    in_specs = [face_spec(d) for d in range(6)] + [
        full3(halos[0].shape),
        full3(halos[1].shape),
        full3(halos[2].shape),
        full3(halos[3].shape),
        tile3(coup.shape[1:]),
        tile3(p_hi.shape[1:]),
        tile3(p_lo.shape[1:]),
        full2(landed.shape),
        tile3(inv.shape[1:]),
    ]
    operands = [faces4] * 6 + [*halos, coup, p_hi, p_lo, landed, inv]
    out_shape = [jax.ShapeDtypeStruct((tiles, rows, cols), BF16)]
    out_specs = [tile3((rows, cols))]
    scratch = [pltpu.VMEM((6 * 48, cols), BF16)]
    if with_message:
        in_specs += [full2(sel.shape), tile3(pt_hi.shape[1:]), tile3(pt_lo.shape[1:])]
        operands += [sel, pt_hi, pt_lo]
        out_shape.append(jax.ShapeDtypeStruct((slots, cols), BF16))
        out_specs.append(full2((slots, cols)))
        shapes, specs = face_outputs(sx, sy, sz, cols)
        out_shape += shapes
        out_specs += specs
        scratch.append(pltpu.VMEM((slots, cols), F32))
    result = pl.pallas_call(
        make_step_kernel(sx, sy, sz, with_message),
        grid=(tiles,),
        in_specs=in_specs,
        out_specs=out_specs,
        out_shape=out_shape,
        scratch_shapes=scratch,
        compiler_params=pltpu.CompilerParams(
            dimension_semantics=("arbitrary",), vmem_limit_bytes=48 * 1024 * 1024
        ),
    )(*operands)
    new = result[0].reshape(shape)
    if not with_message:
        return new, None, None, None
    return new, result[1], result[2], list(result[3:7])


def exchange(values):
    return lax.all_to_all(values, ("gx", "gy"), split_axis=0, concat_axis=0, tiled=True)


def split(values):
    hi = values.astype(BF16)
    lo = (values - hi.astype(F32)).astype(BF16)
    return hi, lo


def local(
    later_adjoint,
    coupling,
    inverse_diag,
    tile_mask,
    perf_cell,
    perf_slot,
    perf_live,
    perf_coef,
    well_gain,
    misfit,
):
    sx, sy, sz, rows, cols = later_adjoint.shape
    tiles = sx * sy * sz
    slot_count = perf_cell.shape[1]
    peers = slot_count // CAPACITY
    wells_here = well_gain.shape[0]
    axes = ("gx", "gy")

    mask = tile_mask.astype(BF16).reshape(tiles, 6)
    coup = coupling.reshape(tiles, 6, rows, 48) * mask[:, :, None, None]
    coup = coup.transpose(0, 2, 1, 3).reshape(tiles, rows, 6 * 48)
    inv = inverse_diag.reshape(tiles, rows, rows)
    sel = jnp.asarray(selection().reshape(288, 192), BF16)

    in_use = perf_live[0].astype(F32)
    cell_ids = perf_cell[0]
    tile_of = cell_ids // 64
    cell_of = cell_ids % 64
    weights = [perf_coef[component, 0] * in_use for component in range(3)]

    def placement(slot_last):
        tile_ids = jnp.arange(tiles, dtype=jnp.int32)[:, None, None]
        if slot_last:
            unk_ids = jnp.arange(rows, dtype=jnp.int32)[None, :, None]
            pick = lambda v: v[None, None, :]
        else:
            unk_ids = jnp.arange(rows, dtype=jnp.int32)[None, None, :]
            pick = lambda v: v[None, :, None]
        place = 0.0
        for component in range(3):
            hit = (tile_ids == pick(tile_of)) & (unk_ids == pick(component * 64 + cell_of))
            place = place + jnp.where(hit, pick(weights[component]), 0.0)
        return split(place)

    p_hi, p_lo = placement(True)
    pt_hi, pt_lo = placement(False)

    slot_tag = perf_slot[0].astype(BF16).reshape(peers, CAPACITY, 1)
    well_index = jnp.arange(wells_here, dtype=jnp.int32).astype(BF16)

    adjoint = later_adjoint
    faces, sides = all_faces(later_adjoint, sel)
    flat0 = later_adjoint.reshape(tiles, rows, cols)
    message = (
        jnp.einsum("tup,tuc->pc", p_hi, flat0, preferred_element_type=F32)
        + jnp.einsum("tup,tuc->pc", p_lo, flat0, preferred_element_type=F32)
    ).astype(BF16)
    collected = []
    for sweep_index in range(STEPS):
        halos = send_faces(sides)
        payload = message.reshape(peers, CAPACITY, cols)
        if sweep_index == 0:
            tags = jnp.broadcast_to(slot_tag, (peers, CAPACITY, 128))
            payload = jnp.concatenate([payload, tags], axis=2)
        arrived = exchange(payload)
        if sweep_index == 0:
            arrived_tags = arrived[:, :, cols]
            selector = (arrived_tags.reshape(1, slot_count) == well_index[:, None]).astype(BF16)
        arrived = arrived[:, :, :cols]
        summed = jnp.dot(selector, arrived.reshape(slot_count, cols), preferred_element_type=F32)
        well_adj = (well_gain[:, None] * (summed + misfit[sweep_index])).astype(BF16)
        returned = jnp.einsum("ws,wr->sr", selector, well_adj, preferred_element_type=F32).astype(BF16)
        landed = exchange(returned.reshape(peers, CAPACITY, cols)).reshape(slot_count, cols)
        last = sweep_index == STEPS - 1
        adjoint, message, faces, sides = step_call(
            later_adjoint.shape, faces, halos, coup, sel, p_hi, p_lo, landed, inv, pt_hi, pt_lo, not last
        )
        collected.append(well_adj)
    return (adjoint, jnp.stack(collected))


def solution(mesh):
    return jax.shard_map(
        local,
        mesh=mesh,
        in_specs=(
            P("gx", "gy", None, None, None),
            P("gx", "gy", None, None, None, None),
            P("gx", "gy", None, None, None),
            P("gx", "gy", None, None),
            P(("gx", "gy"), None),
            P(("gx", "gy"), None),
            P(("gx", "gy"), None),
            P(None, ("gx", "gy"), None),
            P(("gx", "gy")),
            P(None, ("gx", "gy"), None),
        ),
        out_specs=(P("gx", "gy", None, None, None), P(None, ("gx", "gy"), None)),
        check_vma=False,
    )
```

```python
import numpy as np
import jax
import jax.numpy as jnp
from jax import lax
from jax.experimental import pallas as pl
from jax.experimental.pallas import tpu as pltpu
from jax.sharding import PartitionSpec as P


CAPACITY = 2
STEPS = 2
F32 = jnp.float32
BF16 = jnp.bfloat16


def face_rows():
    rows = np.zeros((6, 48), np.int32)
    for k in range(3):
        for p in range(4):
            for q in range(4):
                f = 16 * k + 4 * p + q
                rows[0, f] = 64 * k + 16 * 3 + 4 * p + q
                rows[1, f] = 64 * k + 4 * p + q
                rows[2, f] = 64 * k + 16 * p + 4 * 3 + q
                rows[3, f] = 64 * k + 16 * p + q
                rows[4, f] = 64 * k + 16 * p + 4 * q + 3
                rows[5, f] = 64 * k + 16 * p + 4 * q
    return rows


FACE_ROWS = face_rows()


def selection():
    sel = np.zeros((6, 48, 192), np.float32)
    for d in range(6):
        sel[d, np.arange(48), FACE_ROWS[d]] = 1.0
    return sel


def tile_coords(t, sy, sz):
    return t // (sy * sz), (t // sz) % sy, t % sz


def emit_halos(faces, a, b, c, sx, sy, sz, refs):
    ux_ref, dx_ref, uy_ref, dy_ref = refs
    cases = (
        (a == sx - 1, ux_ref, b * sz + c, 0),
        (a == 0, dx_ref, b * sz + c, 1),
        (b == sy - 1, uy_ref, a * sz + c, 2),
        (b == 0, dy_ref, a * sz + c, 3),
    )
    for on_side, ref, slot, d in cases:

        @pl.when(on_side)
        def _():
            ref[slot] = faces[48 * d : 48 * d + 48]


def face_outputs(sx, sy, sz, cols):
    tiles = sx * sy * sz
    shapes = [(sy * sz, 48, cols), (sy * sz, 48, cols), (sx * sz, 48, cols), (sx * sz, 48, cols)]
    specs = [pl.BlockSpec(shape, lambda t: (0, 0, 0)) for shape in shapes]
    out_shape = [jax.ShapeDtypeStruct((tiles, 288, cols), BF16)]
    out_specs = [pl.BlockSpec((1, 288, cols), lambda t: (t, 0, 0))]
    out_shape += [jax.ShapeDtypeStruct(shape, BF16) for shape in shapes]
    return out_shape, out_specs + specs


def faces_kernel(sx, sy, sz):
    def kernel(a_ref, sel_ref, of_ref, *refs):
        t = pl.program_id(0)
        a, b, c = tile_coords(t, sy, sz)
        faces = jnp.dot(sel_ref[...], a_ref[0], preferred_element_type=F32).astype(BF16)
        of_ref[0] = faces
        emit_halos(faces, a, b, c, sx, sy, sz, refs)

    return kernel


def all_faces(adjoint, sel):
    sx, sy, sz, rows, cols = adjoint.shape
    tiles = sx * sy * sz
    out_shape, out_specs = face_outputs(sx, sy, sz, cols)
    result = pl.pallas_call(
        faces_kernel(sx, sy, sz),
        grid=(tiles,),
        in_specs=[pl.BlockSpec((1, rows, cols), lambda t: (t, 0, 0)), pl.BlockSpec(sel.shape, lambda t: (0, 0))],
        out_specs=out_specs,
        out_shape=out_shape,
        compiler_params=pltpu.CompilerParams(dimension_semantics=("arbitrary",)),
    )(adjoint.reshape(tiles, rows, cols), sel)
    return result[0], list(result[1:])


def send_faces(sides):
    out = []
    for axis, up_part, down_part in (("gx", sides[0], sides[1]), ("gy", sides[2], sides[3])):
        count = lax.axis_size(axis)
        up = [(i, i + 1) for i in range(count - 1)]
        down = [(j, i) for i, j in up]
        out.append(lax.ppermute(up_part, axis, up))
        out.append(lax.ppermute(down_part, axis, down))
    return out


def neighbour_of(t, d, sx, sy, sz):
    a, b, c = tile_coords(t, sy, sz)
    per_x = sy * sz
    table = (
        (a > 0, t - per_x),
        (a < sx - 1, t + per_x),
        (b > 0, t - sz),
        (b < sy - 1, t + sz),
        (c > 0, t - 1),
        (c < sz - 1, t + 1),
    )
    inside, nb = table[d]
    return inside, jnp.clip(nb, 0, sx * sy * sz - 1)


def make_step_kernel(sx, sy, sz, with_message):
    def kernel(*refs):
        face_refs = refs[:6]
        hxm_ref, hxp_ref, hym_ref, hyp_ref, coup_ref, phi_ref, plo_ref, landed_ref, inv_ref = refs[6:15]
        rest = refs[15:]
        if with_message:
            sel_ref, pthi_ref, ptlo_ref, out_ref, msg_ref, of_ref = rest[:6]
            side_refs = rest[6:10]
            faces_ref, acc_ref = rest[10:]
        else:
            out_ref, faces_ref = rest
        t = pl.program_id(0)
        a, b, c = tile_coords(t, sy, sz)
        zero = jnp.zeros((48, faces_ref.shape[-1]), BF16)
        halos = (
            (hxm_ref, b * sz + c),
            (hxp_ref, b * sz + c),
            (hym_ref, a * sz + c),
            (hyp_ref, a * sz + c),
            (None, None),
            (None, None),
        )
        for d in range(6):
            inside, _ = neighbour_of(t, d, sx, sy, sz)
            halo, slot = halos[d]
            src = face_refs[d]

            @pl.when(inside)
            def _():
                faces_ref[pl.ds(48 * d, 48), :] = src[0, 0]

            @pl.when(jnp.logical_not(inside))
            def _():
                faces_ref[pl.ds(48 * d, 48), :] = zero if halo is None else halo[slot]

        rows = coup_ref.shape[1]
        flux = jnp.dot(coup_ref[0], faces_ref[...], preferred_element_type=F32)
        half = landed_ref.shape[1] // 2
        landed = jnp.concatenate([landed_ref[:, :half], landed_ref[:, half:]], axis=0)
        both = jnp.dot(jnp.concatenate([phi_ref[0], plo_ref[0]], axis=0), landed, preferred_element_type=F32)
        added = both[:rows] + both[rows:]
        source = (flux + added).astype(BF16)
        new = (-jnp.dot(inv_ref[0], source, preferred_element_type=F32)).astype(BF16)
        out_ref[0] = new
        if with_message:
            n_sel, n_slot = sel_ref.shape[0], pthi_ref.shape[1]
            lhs = jnp.concatenate([sel_ref[...], pthi_ref[0], ptlo_ref[0]], axis=0)
            both = jnp.dot(lhs, new, preferred_element_type=F32)
            faces_new = both[:n_sel].astype(BF16)
            of_ref[0] = faces_new
            emit_halos(faces_new, a, b, c, sx, sy, sz, side_refs)
            part = both[n_sel : n_sel + n_slot] + both[n_sel + n_slot :]

            @pl.when(t == 0)
            def _():
                acc_ref[...] = part

            @pl.when(t > 0)
            def _():
                acc_ref[...] += part

            @pl.when(t == pl.num_programs(0) - 1)
            def _():
                peers, cols = msg_ref.shape[0], acc_ref.shape[1]
                msg_ref[:, :cols] = acc_ref[:peers, :].astype(BF16)
                msg_ref[:, cols:] = acc_ref[peers:, :].astype(BF16)

    return kernel


def step_call(shape, faces, halos, coup, sel, p_hi, p_lo, landed, inv, pt_hi, pt_lo, with_message):
    sx, sy, sz, rows, cols = shape
    tiles = sx * sy * sz
    slots = 2 * landed.shape[0]
    faces4 = faces.reshape(tiles, 6, 48, cols)
    full3 = lambda shape: pl.BlockSpec(shape, lambda t: (0, 0, 0))
    full2 = lambda shape: pl.BlockSpec(shape, lambda t: (0, 0))
    tile3 = lambda shape: pl.BlockSpec((1,) + shape, lambda t: (t, 0, 0))

    def face_spec(d):
        return pl.BlockSpec((1, 1, 48, cols), lambda t: (neighbour_of(t, d, sx, sy, sz)[1], d, 0, 0))

    in_specs = [face_spec(d) for d in range(6)] + [
        full3(halos[0].shape),
        full3(halos[1].shape),
        full3(halos[2].shape),
        full3(halos[3].shape),
        tile3(coup.shape[1:]),
        tile3(p_hi.shape[1:]),
        tile3(p_lo.shape[1:]),
        full2(landed.shape),
        tile3(inv.shape[1:]),
    ]
    operands = [faces4] * 6 + [*halos, coup, p_hi, p_lo, landed, inv]
    out_shape = [jax.ShapeDtypeStruct((tiles, rows, cols), BF16)]
    out_specs = [tile3((rows, cols))]
    scratch = [pltpu.VMEM((6 * 48, cols), BF16)]
    if with_message:
        in_specs += [full2(sel.shape), tile3(pt_hi.shape[1:]), tile3(pt_lo.shape[1:])]
        operands += [sel, pt_hi, pt_lo]
        out_shape.append(jax.ShapeDtypeStruct((slots // 2, 2 * cols), BF16))
        out_specs.append(full2((slots // 2, 2 * cols)))
        shapes, specs = face_outputs(sx, sy, sz, cols)
        out_shape += shapes
        out_specs += specs
        scratch.append(pltpu.VMEM((slots, cols), F32))
    result = pl.pallas_call(
        make_step_kernel(sx, sy, sz, with_message),
        grid=(tiles,),
        in_specs=in_specs,
        out_specs=out_specs,
        out_shape=out_shape,
        scratch_shapes=scratch,
        compiler_params=pltpu.CompilerParams(
            dimension_semantics=("arbitrary",), vmem_limit_bytes=48 * 1024 * 1024
        ),
    )(*operands)
    new = result[0].reshape(shape)
    if not with_message:
        return new, None, None, None
    return new, result[1], result[2], list(result[3:7])


def exchange(values):
    return lax.all_to_all(values, ("gx", "gy"), split_axis=0, concat_axis=0, tiled=True)


def split(values):
    hi = values.astype(BF16)
    lo = (values - hi.astype(F32)).astype(BF16)
    return hi, lo


def local(
    later_adjoint,
    coupling,
    inverse_diag,
    tile_mask,
    perf_cell,
    perf_slot,
    perf_live,
    perf_coef,
    well_gain,
    misfit,
):
    sx, sy, sz, rows, cols = later_adjoint.shape
    tiles = sx * sy * sz
    slot_count = perf_cell.shape[1]
    peers = slot_count // CAPACITY
    wells_here = well_gain.shape[0]
    axes = ("gx", "gy")

    mask = tile_mask.astype(BF16).reshape(tiles, 6)
    coup = coupling.reshape(tiles, 6, rows, 48) * mask[:, :, None, None]
    coup = coup.transpose(0, 2, 1, 3).reshape(tiles, rows, 6 * 48)
    inv = inverse_diag.reshape(tiles, rows, rows)
    sel = jnp.asarray(selection().reshape(288, 192), BF16)

    order = np.concatenate([np.arange(0, slot_count, CAPACITY), np.arange(1, slot_count, CAPACITY)])
    in_use = perf_live[0][order].astype(F32)
    cell_ids = perf_cell[0][order]
    tile_of = cell_ids // 64
    cell_of = cell_ids % 64
    weights = [perf_coef[component, 0][order] * in_use for component in range(3)]

    def placement(slot_last):
        tile_ids = jnp.arange(tiles, dtype=jnp.int32)[:, None, None]
        if slot_last:
            unk_ids = jnp.arange(rows, dtype=jnp.int32)[None, :, None]
            pick = lambda v: v[None, None, :]
        else:
            unk_ids = jnp.arange(rows, dtype=jnp.int32)[None, None, :]
            pick = lambda v: v[None, :, None]
        place = 0.0
        for component in range(3):
            hit = (tile_ids == pick(tile_of)) & (unk_ids == pick(component * 64 + cell_of))
            place = place + jnp.where(hit, pick(weights[component]), 0.0)
        return split(place)

    p_hi, p_lo = placement(True)
    pt_hi, pt_lo = placement(False)

    slot_tag = perf_slot[0].astype(BF16).reshape(peers, CAPACITY)
    slot_tag = jnp.concatenate([slot_tag, jnp.zeros((peers, 128 - CAPACITY), BF16)], axis=1)
    well_index = jnp.arange(wells_here, dtype=jnp.int32).astype(BF16)

    adjoint = later_adjoint
    faces, sides = all_faces(later_adjoint, sel)
    flat0 = later_adjoint.reshape(tiles, rows, cols)
    message = (
        jnp.einsum("tup,tuc->pc", p_hi, flat0, preferred_element_type=F32)
        + jnp.einsum("tup,tuc->pc", p_lo, flat0, preferred_element_type=F32)
    ).astype(BF16)
    message = jnp.concatenate([message[:peers], message[peers:]], axis=1)
    collected = []
    for sweep_index in range(STEPS):
        halos = send_faces(sides)
        payload = message
        if sweep_index == 0:
            payload = jnp.concatenate([payload, slot_tag], axis=1)
        arrived = exchange(payload)
        if sweep_index == 0:
            arrived_tags = arrived[:, 2 * cols : 2 * cols + CAPACITY].T.reshape(1, slot_count)
            selector = (arrived_tags == well_index[:, None]).astype(BF16)
        arrived = jnp.concatenate([arrived[:, :cols], arrived[:, cols : 2 * cols]], axis=0)
        summed = jnp.dot(selector, arrived, preferred_element_type=F32)
        well_adj = (well_gain[:, None] * (summed + misfit[sweep_index])).astype(BF16)
        returned = jnp.einsum("ws,wr->sr", selector, well_adj, preferred_element_type=F32).astype(BF16)
        landed = exchange(jnp.concatenate([returned[:peers], returned[peers:]], axis=1))
        last = sweep_index == STEPS - 1
        adjoint, message, faces, sides = step_call(
            later_adjoint.shape, faces, halos, coup, sel, p_hi, p_lo, landed, inv, pt_hi, pt_lo, not last
        )
        collected.append(well_adj)
    return (adjoint, jnp.stack(collected))


def solution(mesh):
    return jax.shard_map(
        local,
        mesh=mesh,
        in_specs=(
            P("gx", "gy", None, None, None),
            P("gx", "gy", None, None, None, None),
            P("gx", "gy", None, None, None),
            P("gx", "gy", None, None),
            P(("gx", "gy"), None),
            P(("gx", "gy"), None),
            P(("gx", "gy"), None),
            P(None, ("gx", "gy"), None),
            P(("gx", "gy")),
            P(None, ("gx", "gy"), None),
        ),
        out_specs=(P("gx", "gy", None, None, None), P(None, ("gx", "gy"), None)),
        check_vma=False,
    )
```

```python
import numpy as np
import jax
import jax.numpy as jnp
from jax import lax
from jax.experimental import pallas as pl
from jax.experimental.pallas import tpu as pltpu
from jax.sharding import PartitionSpec as P


CAPACITY = 2
STEPS = 2
F32 = jnp.float32
BF16 = jnp.bfloat16


def face_rows():
    rows = np.zeros((6, 48), np.int32)
    for k in range(3):
        for p in range(4):
            for q in range(4):
                f = 16 * k + 4 * p + q
                rows[0, f] = 64 * k + 16 * 3 + 4 * p + q
                rows[1, f] = 64 * k + 4 * p + q
                rows[2, f] = 64 * k + 16 * p + 4 * 3 + q
                rows[3, f] = 64 * k + 16 * p + q
                rows[4, f] = 64 * k + 16 * p + 4 * q + 3
                rows[5, f] = 64 * k + 16 * p + 4 * q
    return rows


FACE_ROWS = face_rows()


def selection():
    sel = np.zeros((6, 48, 192), np.float32)
    for d in range(6):
        sel[d, np.arange(48), FACE_ROWS[d]] = 1.0
    return sel


def tile_coords(t, sy, sz):
    return t // (sy * sz), (t // sz) % sy, t % sz


def emit_halos(faces, a, b, c, sx, sy, sz, refs):
    ux_ref, dx_ref, uy_ref, dy_ref = refs
    cases = (
        (a == sx - 1, ux_ref, b * sz + c, 0),
        (a == 0, dx_ref, b * sz + c, 1),
        (b == sy - 1, uy_ref, a * sz + c, 2),
        (b == 0, dy_ref, a * sz + c, 3),
    )
    for on_side, ref, slot, d in cases:

        @pl.when(on_side)
        def _():
            ref[slot] = faces[48 * d : 48 * d + 48]


def face_outputs(sx, sy, sz, cols):
    tiles = sx * sy * sz
    shapes = [(sy * sz, 48, cols), (sy * sz, 48, cols), (sx * sz, 48, cols), (sx * sz, 48, cols)]
    specs = [pl.BlockSpec(shape, lambda t: (0, 0, 0)) for shape in shapes]
    out_shape = [jax.ShapeDtypeStruct((tiles, 288, cols), BF16)]
    out_specs = [pl.BlockSpec((1, 288, cols), lambda t: (t, 0, 0))]
    out_shape += [jax.ShapeDtypeStruct(shape, BF16) for shape in shapes]
    return out_shape, out_specs + specs


def faces_kernel(sx, sy, sz):
    def kernel(a_ref, sel_ref, of_ref, *refs):
        t = pl.program_id(0)
        a, b, c = tile_coords(t, sy, sz)
        faces = jnp.dot(sel_ref[...], a_ref[0], preferred_element_type=F32).astype(BF16)
        of_ref[0] = faces
        emit_halos(faces, a, b, c, sx, sy, sz, refs)

    return kernel


def all_faces(adjoint, sel):
    sx, sy, sz, rows, cols = adjoint.shape
    tiles = sx * sy * sz
    out_shape, out_specs = face_outputs(sx, sy, sz, cols)
    result = pl.pallas_call(
        faces_kernel(sx, sy, sz),
        grid=(tiles,),
        in_specs=[pl.BlockSpec((1, rows, cols), lambda t: (t, 0, 0)), pl.BlockSpec(sel.shape, lambda t: (0, 0))],
        out_specs=out_specs,
        out_shape=out_shape,
        compiler_params=pltpu.CompilerParams(dimension_semantics=("arbitrary",)),
    )(adjoint.reshape(tiles, rows, cols), sel)
    return result[0], list(result[1:])


def send_faces(sides):
    out = []
    for axis, up_part, down_part in (("gx", sides[0], sides[1]), ("gy", sides[2], sides[3])):
        count = lax.axis_size(axis)
        up = [(i, i + 1) for i in range(count - 1)]
        down = [(j, i) for i, j in up]
        out.append(lax.ppermute(up_part, axis, up))
        out.append(lax.ppermute(down_part, axis, down))
    return out


def neighbour_of(t, d, sx, sy, sz):
    a, b, c = tile_coords(t, sy, sz)
    per_x = sy * sz
    table = (
        (a > 0, t - per_x),
        (a < sx - 1, t + per_x),
        (b > 0, t - sz),
        (b < sy - 1, t + sz),
        (c > 0, t - 1),
        (c < sz - 1, t + 1),
    )
    inside, nb = table[d]
    return inside, jnp.clip(nb, 0, sx * sy * sz - 1)


def make_step_kernel(sx, sy, sz, with_message):
    def kernel(*refs):
        face_refs = refs[:6]
        hxm_ref, hxp_ref, hym_ref, hyp_ref, coup_ref, phi_ref, plo_ref, landed_ref, inv_ref = refs[6:15]
        rest = refs[15:]
        if with_message:
            sel_ref, pthi_ref, ptlo_ref, out_ref, msg_ref, of_ref = rest[:6]
            side_refs = rest[6:10]
            faces_ref, added_ref, acc_ref = rest[10:]
        else:
            out_ref, faces_ref, added_ref = rest
        t = pl.program_id(0)
        a, b, c = tile_coords(t, sy, sz)
        zero = jnp.zeros((48, faces_ref.shape[-1]), BF16)
        halos = (
            (hxm_ref, b * sz + c),
            (hxp_ref, b * sz + c),
            (hym_ref, a * sz + c),
            (hyp_ref, a * sz + c),
            (None, None),
            (None, None),
        )
        for d in range(6):
            inside, _ = neighbour_of(t, d, sx, sy, sz)
            halo, slot = halos[d]
            src = face_refs[d]

            @pl.when(inside)
            def _():
                faces_ref[pl.ds(48 * d, 48), :] = src[0, 0]

            @pl.when(jnp.logical_not(inside))
            def _():
                faces_ref[pl.ds(48 * d, 48), :] = zero if halo is None else halo[slot]

        @pl.when(t == 0)
        def _():
            landed = landed_ref[...]
            whole = jnp.dot(phi_ref[...], landed, preferred_element_type=F32)
            added_ref[...] = whole + jnp.dot(plo_ref[...], landed, preferred_element_type=F32)

        rows = coup_ref.shape[1]
        flux = jnp.dot(coup_ref[0], faces_ref[...], preferred_element_type=F32)
        added = added_ref[pl.ds(pl.multiple_of(t * rows, 8), rows), :]
        source = (flux + added).astype(BF16)
        new = (-jnp.dot(inv_ref[0], source, preferred_element_type=F32)).astype(BF16)
        out_ref[0] = new
        if with_message:
            n_sel, n_slot = sel_ref.shape[0], pthi_ref.shape[1]
            lhs = jnp.concatenate([sel_ref[...], pthi_ref[0], ptlo_ref[0]], axis=0)
            both = jnp.dot(lhs, new, preferred_element_type=F32)
            faces_new = both[:n_sel].astype(BF16)
            of_ref[0] = faces_new
            emit_halos(faces_new, a, b, c, sx, sy, sz, side_refs)
            part = both[n_sel : n_sel + n_slot] + both[n_sel + n_slot :]

            @pl.when(t == 0)
            def _():
                acc_ref[...] = part

            @pl.when(t > 0)
            def _():
                acc_ref[...] += part

            @pl.when(t == pl.num_programs(0) - 1)
            def _():
                msg_ref[...] = acc_ref[...].astype(BF16)

    return kernel


def step_call(shape, faces, halos, coup, sel, p_hi, p_lo, landed, inv, pt_hi, pt_lo, with_message):
    sx, sy, sz, rows, cols = shape
    tiles = sx * sy * sz
    slots = landed.shape[0]
    faces4 = faces.reshape(tiles, 6, 48, cols)
    full3 = lambda shape: pl.BlockSpec(shape, lambda t: (0, 0, 0))
    full2 = lambda shape: pl.BlockSpec(shape, lambda t: (0, 0))
    tile3 = lambda shape: pl.BlockSpec((1,) + shape, lambda t: (t, 0, 0))

    def face_spec(d):
        return pl.BlockSpec((1, 1, 48, cols), lambda t: (neighbour_of(t, d, sx, sy, sz)[1], d, 0, 0))

    in_specs = [face_spec(d) for d in range(6)] + [
        full3(halos[0].shape),
        full3(halos[1].shape),
        full3(halos[2].shape),
        full3(halos[3].shape),
        tile3(coup.shape[1:]),
        full2((tiles * rows, slots)),
        full2((tiles * rows, slots)),
        full2(landed.shape),
        tile3(inv.shape[1:]),
    ]
    flat_hi = p_hi.reshape(tiles * rows, slots)
    flat_lo = p_lo.reshape(tiles * rows, slots)
    operands = [faces4] * 6 + [*halos, coup, flat_hi, flat_lo, landed, inv]
    out_shape = [jax.ShapeDtypeStruct((tiles, rows, cols), BF16)]
    out_specs = [tile3((rows, cols))]
    scratch = [pltpu.VMEM((6 * 48, cols), BF16), pltpu.VMEM((tiles * rows, cols), F32)]
    if with_message:
        in_specs += [full2(sel.shape), tile3(pt_hi.shape[1:]), tile3(pt_lo.shape[1:])]
        operands += [sel, pt_hi, pt_lo]
        out_shape.append(jax.ShapeDtypeStruct((slots, cols), BF16))
        out_specs.append(full2((slots, cols)))
        shapes, specs = face_outputs(sx, sy, sz, cols)
        out_shape += shapes
        out_specs += specs
        scratch.append(pltpu.VMEM((slots, cols), F32))
    result = pl.pallas_call(
        make_step_kernel(sx, sy, sz, with_message),
        grid=(tiles,),
        in_specs=in_specs,
        out_specs=out_specs,
        out_shape=out_shape,
        scratch_shapes=scratch,
        compiler_params=pltpu.CompilerParams(
            dimension_semantics=("arbitrary",), vmem_limit_bytes=56 * 1024 * 1024
        ),
    )(*operands)
    new = result[0].reshape(shape)
    if not with_message:
        return new, None, None, None
    return new, result[1], result[2], list(result[3:7])


def exchange(values):
    return lax.all_to_all(values, ("gx", "gy"), split_axis=0, concat_axis=0, tiled=True)


def split(values):
    hi = values.astype(BF16)
    lo = (values - hi.astype(F32)).astype(BF16)
    return hi, lo


def local(
    later_adjoint,
    coupling,
    inverse_diag,
    tile_mask,
    perf_cell,
    perf_slot,
    perf_live,
    perf_coef,
    well_gain,
    misfit,
):
    sx, sy, sz, rows, cols = later_adjoint.shape
    tiles = sx * sy * sz
    slot_count = perf_cell.shape[1]
    peers = slot_count // CAPACITY
    wells_here = well_gain.shape[0]
    axes = ("gx", "gy")

    mask = tile_mask.astype(BF16).reshape(tiles, 6)
    coup = coupling.reshape(tiles, 6, rows, 48) * mask[:, :, None, None]
    coup = coup.transpose(0, 2, 1, 3).reshape(tiles, rows, 6 * 48)
    inv = inverse_diag.reshape(tiles, rows, rows)
    sel = jnp.asarray(selection().reshape(288, 192), BF16)

    in_use = perf_live[0].astype(F32)
    cell_ids = perf_cell[0]
    tile_of = cell_ids // 64
    cell_of = cell_ids % 64
    weights = [perf_coef[component, 0] * in_use for component in range(3)]

    def placement(slot_last):
        tile_ids = jnp.arange(tiles, dtype=jnp.int32)[:, None, None]
        if slot_last:
            unk_ids = jnp.arange(rows, dtype=jnp.int32)[None, :, None]
            pick = lambda v: v[None, None, :]
        else:
            unk_ids = jnp.arange(rows, dtype=jnp.int32)[None, None, :]
            pick = lambda v: v[None, :, None]
        place = 0.0
        for component in range(3):
            hit = (tile_ids == pick(tile_of)) & (unk_ids == pick(component * 64 + cell_of))
            place = place + jnp.where(hit, pick(weights[component]), 0.0)
        return split(place)

    p_hi, p_lo = placement(True)
    pt_hi, pt_lo = placement(False)

    slot_tag = perf_slot[0].astype(BF16).reshape(peers, CAPACITY, 1)
    well_index = jnp.arange(wells_here, dtype=jnp.int32).astype(BF16)

    adjoint = later_adjoint
    faces, sides = all_faces(later_adjoint, sel)
    flat0 = later_adjoint.reshape(tiles, rows, cols)
    both = jnp.einsum("tup,tuc->pc", jnp.concatenate([p_hi, p_lo], axis=2), flat0, preferred_element_type=F32)
    message = (both[:slot_count] + both[slot_count:]).astype(BF16)
    collected = []
    for sweep_index in range(STEPS):
        halos = send_faces(sides)
        payload = message.reshape(peers, CAPACITY, cols)
        if sweep_index == 0:
            tags = jnp.broadcast_to(slot_tag, (peers, CAPACITY, 128))
            payload = jnp.concatenate([payload, tags], axis=2)
        arrived = exchange(payload)
        if sweep_index == 0:
            arrived_tags = arrived[:, :, cols]
            selector = (arrived_tags.reshape(1, slot_count) == well_index[:, None]).astype(BF16)
        arrived = arrived[:, :, :cols]
        summed = jnp.dot(selector, arrived.reshape(slot_count, cols), preferred_element_type=F32)
        well_adj = (well_gain[:, None] * (summed + misfit[sweep_index])).astype(BF16)
        returned = jnp.einsum("ws,wr->sr", selector, well_adj, preferred_element_type=F32).astype(BF16)
        landed = exchange(returned.reshape(peers, CAPACITY, cols)).reshape(slot_count, cols)
        last = sweep_index == STEPS - 1
        adjoint, message, faces, sides = step_call(
            later_adjoint.shape, faces, halos, coup, sel, p_hi, p_lo, landed, inv, pt_hi, pt_lo, not last
        )
        collected.append(well_adj)
    return (adjoint, jnp.stack(collected))


def solution(mesh):
    return jax.shard_map(
        local,
        mesh=mesh,
        in_specs=(
            P("gx", "gy", None, None, None),
            P("gx", "gy", None, None, None, None),
            P("gx", "gy", None, None, None),
            P("gx", "gy", None, None),
            P(("gx", "gy"), None),
            P(("gx", "gy"), None),
            P(("gx", "gy"), None),
            P(None, ("gx", "gy"), None),
            P(("gx", "gy")),
            P(None, ("gx", "gy"), None),
        ),
        out_specs=(P("gx", "gy", None, None, None), P(None, ("gx", "gy"), None)),
        check_vma=False,
    )
```
